32 devices in a mesh: groups: 2 (over y), rows: 4 (over x, core), rep: 4 (over z).
Axes of the slice: x: 2, y: 2, z: 4, core: 2. Of those that a mesh axis runs over, the one named last changes fastest.
Arguments:
- images: bfloat16 [8, 64, 128, 256], P(('groups', 'rep'), 'rows'), parts along dimension 0, may hold values from -6 to 6
- cotangent: bfloat16 [8, 64, 128, 256], P(('groups', 'rep'), 'rows'), parts along dimension 0, may hold values from -6 to 6
- row_taps: float32 [102, 256], P('groups'), parts along dimension 0, may hold values from -0.875 to 0.875
- col_taps: float32 [102, 256], P('groups'), parts along dimension 0, may hold values from -0.875 to 0.875
- norm_gain: float32 [512], P('groups'), parts along dimension 0, may hold values from 0.25 to 1.75
- norm_shift: float32 [512], P('groups'), parts along dimension 0, may hold values from -3 to 3
- up_weight: bfloat16 [512, 1024], P('groups'), parts along dimension 0, may hold values from -0.375 to 0.375
- up_bias: float32 [2048], P('groups'), parts along dimension 0, may hold values from -3 to 3
- down_weight: bfloat16 [2048, 256], P('groups'), parts along dimension 0, may hold values from -0.1875 to 0.1875
- down_bias: float32 [512], P('groups'), parts along dimension 0, may hold values from -3 to 3
- layer_scale: float32 [512], P('groups'), parts along dimension 0, may hold values from 0.5 to 1.5
Outputs:
- block_out: bfloat16 [8, 64, 128, 256], P(('groups', 'rep'), 'rows'), parts along dimension 0
- image_grad: bfloat16 [8, 64, 128, 256], P(('groups', 'rep'), 'rows'), parts along dimension 0
- row_taps_grad: float32 [102, 256], P('groups'), parts along dimension 0
- col_taps_grad: float32 [102, 256], P('groups'), parts along dimension 0
- scale_grad: float32 [512], P('groups'), parts along dimension 0
- down_bias_grad: float32 [512], P('groups'), parts along dimension 0
- down_grad: float32 [2048, 256], P('groups'), parts along dimension 0
- up_bias_grad: float32 [2048], P('groups'), parts along dimension 0
- up_grad: float32 [512, 1024], P('groups'), parts along dimension 0
- gain_grad: float32 [512], P('groups'), parts along dimension 0
- shift_grad: float32 [512], P('groups'), parts along dimension 0
The draws below stay inside these ranges and needn't reach their ends.
There are 2 independent parts, one for each index of `groups`. The reference program is written for one: setup_inputs(seed, part) draws one part's arguments, and reference() takes and returns one part's arrays. A program takes and returns all parts, laid end to end along the dimension named above; each array names one. Nothing has to cross between parts.
All inputs are finite; a program needn't handle non-finite values.
Results may differ from the reference program's by a relative error of at most 0.0086.
Values may be sent and summed in bfloat16 or wider, within the bound.
No kernel may reach another device: no remote copies, remote signals or barrier semaphores. Data moves between devices by JAX's collectives and lax.ppermute only.
A program may use at most 64 MiB of HBM per device.

```python
import math
import jax
import jax.numpy as jnp
from jax import lax

C = 256
HID = 1024
K = 51
W = 128
H = 64
TILES = 4


def block_scale(rng, shape, split, smallest, high):
    def one(axis_at, blocks):
        draws = jax.random.uniform(jax.random.fold_in(jax.random.fold_in(rng, 6), axis_at), (blocks,), jnp.float32, smallest / len(split), high / len(split))
        return jnp.repeat(jnp.exp(draws), shape[axis_at] // blocks).reshape((-1,) + (1,) * (len(shape) - axis_at - 1))

    loudness = one(*split[0])
    for cut in split[1:]:
        loudness = loudness * one(*cut)
    return loudness


def noise(rng, shape, deviation, bound, shards=(), kind=jnp.bfloat16):
    factor_of = block_scale(rng, shape, shards, -0.22, 0.18) if shards else 1.0
    values = jax.random.normal(rng, shape, jnp.float32) * deviation * factor_of
    return jnp.minimum(jnp.maximum(values, -bound), bound).astype(kind)


def setup_inputs(seed: int = 0, part: int = 0) -> dict:
    arg_keys = jax.random.split(jax.random.key(seed), 12)
    own_keys = jax.random.split(jax.random.fold_in(arg_keys[11], part), 12)
    return {
        "images": noise(own_keys[0], (TILES, H, W, C), 1.0, 6.0, ((0, 4), (1, 4))),
        "cotangent": noise(own_keys[1], (TILES, H, W, C), 1.0, 6.0, ((0, 4), (1, 4))),
        "row_taps": noise(own_keys[2], (K, C), K ** -0.5, 0.875, (), jnp.float32),
        "col_taps": noise(own_keys[3], (K, C), K ** -0.5, 0.875, (), jnp.float32),
        "norm_gain": jnp.clip(1.0 + 0.15 * jax.random.normal(own_keys[4], (C,), jnp.float32), 0.25, 1.75),
        "norm_shift": noise(own_keys[5], (C,), 0.5, 3.0, (), jnp.float32),
        "up_weight": noise(own_keys[6], (C, HID), C ** -0.5, 0.375),
        "up_bias": noise(own_keys[7], (HID,), 0.5, 3.0, (), jnp.float32),
        "down_weight": noise(own_keys[8], (HID, C), HID ** -0.5, 0.1875),
        "down_bias": noise(own_keys[9], (C,), 0.5, 3.0, (), jnp.float32),
        "layer_scale": jnp.clip(jax.random.uniform(own_keys[10], (C,), jnp.float32, 0.5, 1.5), 0.5, 1.5),
    }


EPSILON = 1e-06
CUBIC_TERM = 0.044715
TANH_SCALE = 0.7978845608028654

def activate(pre_act):
    return 0.5 * pre_act * (1.0 + jnp.tanh(TANH_SCALE * (pre_act + CUBIC_TERM * pre_act * pre_act * pre_act)))

def activate_slope(pre_act):
    inner = jnp.tanh(TANH_SCALE * (pre_act + CUBIC_TERM * pre_act * pre_act * pre_act))
    return 0.5 * (1.0 + inner) + 0.5 * pre_act * (1.0 - inner * inner) * TANH_SCALE * (1.0 + 3.0 * CUBIC_TERM * pre_act * pre_act)

def pad_along(source, direction, half_reach):
    widths = [(0, 0)] * source.ndim
    widths[direction] = (half_reach, half_reach)
    return jnp.pad(source, widths)

def slide_padded(padded, taps_table, direction, length):
    shape_out = padded.shape[:direction] + (length,) + padded.shape[direction + 1:]
    result = jnp.zeros(shape_out, jnp.float32)
    for offset in range(taps_table.shape[0]):
        result = result + taps_table[offset] * lax.slice_in_dim(padded, offset, offset + length, axis=direction)
    return result

def tap_sums(cot_field, padded, taps_count, direction):
    length = cot_field.shape[direction]
    lead_axes = tuple(range(cot_field.ndim - 1))
    return jnp.stack([lax.optimization_barrier(jnp.sum(cot_field * lax.slice_in_dim(padded, offset, offset + length, axis=direction), axis=lead_axes)) for offset in range(taps_count)])

def pointwise(mix_rows, image_rows, cot_rows, norm_gain, norm_shift, up_weight, up_bias, down_weight, down_bias, layer_scale):
    mix_float = mix_rows.astype(jnp.float32)
    centered = mix_float - lax.optimization_barrier(jnp.mean(mix_float, axis=-1, keepdims=True))
    inv_dev = lax.rsqrt(lax.optimization_barrier(jnp.mean(centered * centered, axis=-1, keepdims=True)) + EPSILON)
    standardized = centered * inv_dev
    normed = (standardized * norm_gain + norm_shift).astype(jnp.bfloat16)
    pre_act = jnp.dot(normed, up_weight, preferred_element_type=jnp.float32) + up_bias
    activated = activate(pre_act).astype(jnp.bfloat16)
    branch = jnp.dot(activated, down_weight, preferred_element_type=jnp.float32) + down_bias
    cot_float = cot_rows.astype(jnp.float32)
    block_rows = (image_rows.astype(jnp.float32) + layer_scale * branch).astype(jnp.bfloat16)
    branch_cot = cot_float * layer_scale
    branch_grad = branch_cot.astype(jnp.bfloat16)
    act_cot = lax.dot_general(branch_grad, down_weight, (((1,), (1,)), ((), ())), preferred_element_type=jnp.float32)
    pre_cot = act_cot * activate_slope(pre_act)
    pre_grad = pre_cot.astype(jnp.bfloat16)
    normed_cot = lax.dot_general(pre_grad, up_weight, (((1,), (1,)), ((), ())), preferred_element_type=jnp.float32)
    scaled_cot = normed_cot * norm_gain
    grad_rows = (inv_dev * (scaled_cot - lax.optimization_barrier(jnp.mean(scaled_cot, axis=-1, keepdims=True)) - standardized * lax.optimization_barrier(jnp.mean(scaled_cot * standardized, axis=-1, keepdims=True)))).astype(jnp.bfloat16)
    partials = (lax.optimization_barrier(jnp.sum(cot_float * branch, axis=0)), lax.optimization_barrier(jnp.sum(branch_cot, axis=0)), lax.dot_general(activated, branch_grad, (((0,), (0,)), ((), ())), preferred_element_type=jnp.float32), lax.optimization_barrier(jnp.sum(pre_cot, axis=0)), lax.dot_general(normed, pre_grad, (((0,), (0,)), ((), ())), preferred_element_type=jnp.float32), lax.optimization_barrier(jnp.sum(normed_cot * standardized, axis=0)), lax.optimization_barrier(jnp.sum(normed_cot, axis=0)))
    return (block_rows, grad_rows, partials)

def reference(images, cotangent, row_taps, col_taps, norm_gain, norm_shift, up_weight, up_bias, down_weight, down_bias, layer_scale):
    taps_count = row_taps.shape[0]
    half_reach = (taps_count - 1) // 2

    def tile_pass(pair):
        image_tile, cot_tile = pair
        heights, columns, channels = image_tile.shape
        image_padded = pad_along(image_tile.astype(jnp.float32), 1, half_reach)
        row_mix = slide_padded(image_padded, row_taps, 1, columns).astype(jnp.bfloat16)
        row_mix = lax.optimization_barrier(row_mix)
        mix_padded = pad_along(row_mix.astype(jnp.float32), 0, half_reach)
        col_mix = slide_padded(mix_padded, col_taps, 0, heights).astype(jnp.bfloat16)
        col_mix = lax.optimization_barrier(col_mix)
        block_rows, grad_rows, partials = pointwise(col_mix.reshape(-1, channels), image_tile.reshape(-1, channels), cot_tile.reshape(-1, channels), norm_gain, norm_shift, up_weight, up_bias, down_weight, down_bias, layer_scale)
        grad_rows = lax.optimization_barrier(grad_rows)
        col_grad = grad_rows.reshape(image_tile.shape).astype(jnp.float32)
        col_part = tap_sums(col_grad, mix_padded, taps_count, 0)
        row_grad = slide_padded(pad_along(col_grad, 0, half_reach), col_taps[::-1], 0, heights).astype(jnp.bfloat16)
        row_grad = lax.optimization_barrier(row_grad)
        row_float = row_grad.astype(jnp.float32)
        row_part = tap_sums(row_float, image_padded, taps_count, 1)
        image_grad = (cot_tile.astype(jnp.float32) + slide_padded(pad_along(row_float, 1, half_reach), row_taps[::-1], 1, columns)).astype(jnp.bfloat16)
        return (block_rows.reshape(image_tile.shape), image_grad, row_part, col_part) + partials
    outcome = lax.map(tile_pass, (images, cotangent))
    block_out, image_grad, row_parts, col_parts, scale_parts, down_bias_parts, down_parts, up_bias_parts, up_parts, gain_parts, shift_parts = outcome
    pixel_scale = 1.0 / math.sqrt(TILES * H * W)
    return (block_out, image_grad, lax.optimization_barrier(jnp.sum(row_parts, axis=0)) * pixel_scale, lax.optimization_barrier(jnp.sum(col_parts, axis=0)) * pixel_scale, lax.optimization_barrier(jnp.sum(scale_parts, axis=0)) * pixel_scale, lax.optimization_barrier(jnp.sum(down_bias_parts, axis=0)) * pixel_scale, lax.optimization_barrier(jnp.sum(down_parts, axis=0)) * pixel_scale, lax.optimization_barrier(jnp.sum(up_bias_parts, axis=0)) * pixel_scale, lax.optimization_barrier(jnp.sum(up_parts, axis=0)) * pixel_scale, lax.optimization_barrier(jnp.sum(gain_parts, axis=0)) * pixel_scale, lax.optimization_barrier(jnp.sum(shift_parts, axis=0)) * pixel_scale)
```

```python
import math

import jax
import jax.numpy as jnp
from jax import lax
from jax.sharding import PartitionSpec as P

EPSILON = 1e-06
CUBIC_TERM = 0.044715
TANH_SCALE = 0.7978845608028654


def activate(pre_act):
    return (
        0.5
        * pre_act
        * (1.0 + jnp.tanh(TANH_SCALE * (pre_act + CUBIC_TERM * pre_act * pre_act * pre_act)))
    )


def activate_slope(pre_act):
    inner = jnp.tanh(TANH_SCALE * (pre_act + CUBIC_TERM * pre_act * pre_act * pre_act))
    return 0.5 * (1.0 + inner) + 0.5 * pre_act * (1.0 - inner * inner) * TANH_SCALE * (
        1.0 + 3.0 * CUBIC_TERM * pre_act * pre_act
    )


def pad_along(source, direction, half_reach):
    widths = [(0, 0)] * source.ndim
    widths[direction] = (half_reach, half_reach)
    return jnp.pad(source, widths)


def slide_padded(padded, taps_table, direction, length):
    shape_out = padded.shape[:direction] + (length,) + padded.shape[direction + 1 :]
    result = jnp.zeros(shape_out, jnp.float32)
    for offset in range(taps_table.shape[0]):
        result = result + taps_table[offset] * lax.slice_in_dim(
            padded, offset, offset + length, axis=direction
        )
    return result


def tap_sums(cot_field, padded, taps_count, direction):
    length = cot_field.shape[direction]
    lead_axes = tuple(range(cot_field.ndim - 1))
    return jnp.stack(
        [
            jnp.sum(
                cot_field * lax.slice_in_dim(padded, offset, offset + length, axis=direction),
                axis=lead_axes,
            )
            for offset in range(taps_count)
        ]
    )


def pointwise(
    mix_rows,
    image_rows,
    cot_rows,
    norm_gain,
    norm_shift,
    up_weight,
    up_bias,
    down_weight,
    down_bias,
    layer_scale,
):
    mix_float = mix_rows.astype(jnp.float32)
    centered = mix_float - jnp.mean(mix_float, axis=-1, keepdims=True)
    inv_dev = lax.rsqrt(jnp.mean(centered * centered, axis=-1, keepdims=True) + EPSILON)
    standardized = centered * inv_dev
    normed = (standardized * norm_gain + norm_shift).astype(jnp.bfloat16)
    pre_act = jnp.dot(normed, up_weight, preferred_element_type=jnp.float32) + up_bias
    activated = activate(pre_act).astype(jnp.bfloat16)
    branch = jnp.dot(activated, down_weight, preferred_element_type=jnp.float32) + down_bias
    cot_float = cot_rows.astype(jnp.float32)
    block_rows = (image_rows.astype(jnp.float32) + layer_scale * branch).astype(jnp.bfloat16)
    branch_cot = cot_float * layer_scale
    branch_grad = branch_cot.astype(jnp.bfloat16)
    act_cot = lax.dot_general(
        branch_grad, down_weight, (((1,), (1,)), ((), ())), preferred_element_type=jnp.float32
    )
    pre_cot = act_cot * activate_slope(pre_act)
    pre_grad = pre_cot.astype(jnp.bfloat16)
    normed_cot = lax.dot_general(
        pre_grad, up_weight, (((1,), (1,)), ((), ())), preferred_element_type=jnp.float32
    )
    scaled_cot = normed_cot * norm_gain
    grad_rows = (
        inv_dev
        * (
            scaled_cot
            - jnp.mean(scaled_cot, axis=-1, keepdims=True)
            - standardized * jnp.mean(scaled_cot * standardized, axis=-1, keepdims=True)
        )
    ).astype(jnp.bfloat16)
    partials = (
        jnp.sum(cot_float * branch, axis=0),
        jnp.sum(branch_cot, axis=0),
        lax.dot_general(
            activated, branch_grad, (((0,), (0,)), ((), ())), preferred_element_type=jnp.float32
        ),
        jnp.sum(pre_cot, axis=0),
        lax.dot_general(
            normed, pre_grad, (((0,), (0,)), ((), ())), preferred_element_type=jnp.float32
        ),
        jnp.sum(normed_cot * standardized, axis=0),
        jnp.sum(normed_cot, axis=0),
    )
    return (block_rows, grad_rows, partials)


def per_device(
    images,
    cotangent,
    row_taps,
    col_taps,
    norm_gain,
    norm_shift,
    up_weight,
    up_bias,
    down_weight,
    down_bias,
    layer_scale,
):
    tiles_here, band_rows, columns, channels = images.shape
    taps_count = row_taps.shape[0]
    half_reach = (taps_count - 1) // 2
    pixel_scale = 1.0 / math.sqrt(
        tiles_here * lax.axis_size("rep") * band_rows * lax.axis_size("rows") * columns
    )
    image_padded = pad_along(images.astype(jnp.float32), 2, half_reach)
    row_mix = slide_padded(image_padded, row_taps, 2, columns).astype(jnp.bfloat16)
    row_mix = lax.optimization_barrier(row_mix)
    mix_columns = lax.all_to_all(row_mix, "rows", split_axis=2, concat_axis=1, tiled=True)
    mix_padded = pad_along(mix_columns.astype(jnp.float32), 1, half_reach)
    col_local = slide_padded(mix_padded, col_taps, 1, mix_columns.shape[1]).astype(jnp.bfloat16)
    col_mix = lax.all_to_all(col_local, "rows", split_axis=1, concat_axis=2, tiled=True)
    col_mix = lax.optimization_barrier(col_mix)
    block_rows, grad_rows, partials = pointwise(
        col_mix.reshape(-1, channels),
        images.reshape(-1, channels),
        cotangent.reshape(-1, channels),
        norm_gain,
        norm_shift,
        up_weight,
        up_bias,
        down_weight,
        down_bias,
        layer_scale,
    )
    scale_part, down_bias_part, down_part, up_bias_part, up_part, gain_part, shift_part = partials
    block_out = block_rows.reshape(images.shape)
    grad_rows = lax.optimization_barrier(grad_rows)
    col_grad = grad_rows.reshape(images.shape)
    grad_columns = lax.all_to_all(col_grad, "rows", split_axis=2, concat_axis=1, tiled=True)
    grad_float = grad_columns.astype(jnp.float32)
    col_part = tap_sums(grad_float, mix_padded, taps_count, 1)
    row_local = slide_padded(
        pad_along(grad_float, 1, half_reach), col_taps[::-1], 1, grad_columns.shape[1]
    ).astype(jnp.bfloat16)
    row_grad = lax.all_to_all(row_local, "rows", split_axis=1, concat_axis=2, tiled=True)
    row_grad = lax.optimization_barrier(row_grad)
    row_float = row_grad.astype(jnp.float32)
    row_part = tap_sums(row_float, image_padded, taps_count, 2)
    image_grad = (
        cotangent.astype(jnp.float32)
        + slide_padded(pad_along(row_float, 2, half_reach), row_taps[::-1], 2, columns)
    ).astype(jnp.bfloat16)
    early = (scale_part, down_bias_part, down_part, up_bias_part, up_part, gain_part, shift_part)
    flat = lax.psum(
        jnp.concatenate([part.reshape(-1) for part in early]) * pixel_scale, ("rows", "rep")
    )
    scale_total, down_bias_total, down_total, up_bias_total, up_total, gain_total, shift_total = (
        split_like(flat, early)
    )
    row_total, col_total = exchange_sum((row_part * pixel_scale, col_part * pixel_scale), ("rows", "rep"))
    return (
        block_out,
        image_grad,
        row_total,
        col_total,
        scale_total,
        down_bias_total,
        down_total,
        up_bias_total,
        up_total,
        gain_total,
        shift_total,
    )


def exchange_sum(parts, axes):
    count = 1
    for axis in axes:
        count *= lax.axis_size(axis)
    flat = jnp.concatenate([part.reshape(-1) for part in parts])
    piece = -(-flat.shape[0] // (count * 128)) * 128
    flat = jnp.pad(flat, (0, piece * count - flat.shape[0]))
    spread = lax.all_to_all(flat.reshape(count, piece), axes, 0, 0, tiled=True)
    mine = jnp.sum(spread, axis=0, keepdims=True)
    whole = lax.all_to_all(jnp.broadcast_to(mine, (count, piece)), axes, 0, 0, tiled=True)
    return split_like(whole.reshape(-1), parts)


def split_like(flat, parts):
    out = []
    at = 0
    for part in parts:
        out.append(flat[at : at + part.size].reshape(part.shape))
        at += part.size
    return tuple(out)


def solution(mesh):
    placed = (
        P(("groups", "rep"), "rows", None, None),
        P(("groups", "rep"), "rows", None, None),
        P("groups", None),
        P("groups", None),
        P("groups"),
        P("groups"),
        P("groups", None),
        P("groups"),
        P("groups", None),
        P("groups"),
        P("groups"),
    )
    return jax.shard_map(
        per_device,
        mesh=mesh,
        in_specs=placed,
        out_specs=(
            P(("groups", "rep"), "rows", None, None),
            P(("groups", "rep"), "rows", None, None),
            P("groups", None),
            P("groups", None),
            P("groups"),
            P("groups"),
            P("groups", None),
            P("groups"),
            P("groups", None),
            P("groups"),
            P("groups"),
        ),
        check_vma=False,
    )
```

```python
import math

import jax
import jax.numpy as jnp
from jax import lax
from jax.sharding import PartitionSpec as P

EPSILON = 1e-06
CUBIC_TERM = 0.044715
TANH_SCALE = 0.7978845608028654


def activate(pre_act):
    return (
        0.5
        * pre_act
        * (1.0 + jnp.tanh(TANH_SCALE * (pre_act + CUBIC_TERM * pre_act * pre_act * pre_act)))
    )


def activate_slope(pre_act):
    inner = jnp.tanh(TANH_SCALE * (pre_act + CUBIC_TERM * pre_act * pre_act * pre_act))
    return 0.5 * (1.0 + inner) + 0.5 * pre_act * (1.0 - inner * inner) * TANH_SCALE * (
        1.0 + 3.0 * CUBIC_TERM * pre_act * pre_act
    )


def pad_along(source, direction, half_reach):
    widths = [(0, 0)] * source.ndim
    widths[direction] = (half_reach, half_reach)
    return jnp.pad(source, widths)


def slide_padded(padded, taps_table, direction, length):
    shape_out = padded.shape[:direction] + (length,) + padded.shape[direction + 1 :]
    result = jnp.zeros(shape_out, jnp.float32)
    for offset in range(taps_table.shape[0]):
        result = result + taps_table[offset] * lax.slice_in_dim(
            padded, offset, offset + length, axis=direction
        )
    return result


def tap_sums(cot_field, padded, taps_count, direction):
    length = cot_field.shape[direction]
    lead_axes = tuple(range(cot_field.ndim - 1))
    return jnp.stack(
        [
            jnp.sum(
                cot_field * lax.slice_in_dim(padded, offset, offset + length, axis=direction),
                axis=lead_axes,
            )
            for offset in range(taps_count)
        ]
    )


def pointwise(
    mix_rows,
    image_rows,
    cot_rows,
    norm_gain,
    norm_shift,
    up_weight,
    up_bias,
    down_weight,
    down_bias,
    layer_scale,
):
    mix_float = mix_rows.astype(jnp.float32)
    centered = mix_float - jnp.mean(mix_float, axis=-1, keepdims=True)
    inv_dev = lax.rsqrt(jnp.mean(centered * centered, axis=-1, keepdims=True) + EPSILON)
    standardized = centered * inv_dev
    normed = (standardized * norm_gain + norm_shift).astype(jnp.bfloat16)
    pre_act = jnp.dot(normed, up_weight, preferred_element_type=jnp.float32) + up_bias
    activated = activate(pre_act).astype(jnp.bfloat16)
    branch = jnp.dot(activated, down_weight, preferred_element_type=jnp.float32) + down_bias
    cot_float = cot_rows.astype(jnp.float32)
    block_rows = (image_rows.astype(jnp.float32) + layer_scale * branch).astype(jnp.bfloat16)
    branch_cot = cot_float * layer_scale
    branch_grad = branch_cot.astype(jnp.bfloat16)
    act_cot = lax.dot_general(
        branch_grad, down_weight, (((1,), (1,)), ((), ())), preferred_element_type=jnp.float32
    )
    pre_cot = act_cot * activate_slope(pre_act)
    pre_grad = pre_cot.astype(jnp.bfloat16)
    normed_cot = lax.dot_general(
        pre_grad, up_weight, (((1,), (1,)), ((), ())), preferred_element_type=jnp.float32
    )
    scaled_cot = normed_cot * norm_gain
    grad_rows = (
        inv_dev
        * (
            scaled_cot
            - jnp.mean(scaled_cot, axis=-1, keepdims=True)
            - standardized * jnp.mean(scaled_cot * standardized, axis=-1, keepdims=True)
        )
    ).astype(jnp.bfloat16)
    partials = (
        jnp.sum(cot_float * branch, axis=0),
        jnp.sum(branch_cot, axis=0),
        lax.dot_general(
            activated, branch_grad, (((0,), (0,)), ((), ())), preferred_element_type=jnp.float32
        ),
        jnp.sum(pre_cot, axis=0),
        lax.dot_general(
            normed, pre_grad, (((0,), (0,)), ((), ())), preferred_element_type=jnp.float32
        ),
        jnp.sum(normed_cot * standardized, axis=0),
        jnp.sum(normed_cot, axis=0),
    )
    return (block_rows, grad_rows, partials)


def per_device(
    images,
    cotangent,
    row_taps,
    col_taps,
    norm_gain,
    norm_shift,
    up_weight,
    up_bias,
    down_weight,
    down_bias,
    layer_scale,
):
    tiles_here, band_rows, columns, channels = images.shape
    taps_count = row_taps.shape[0]
    half_reach = (taps_count - 1) // 2
    pixel_scale = 1.0 / math.sqrt(
        tiles_here * lax.axis_size("rep") * band_rows * lax.axis_size("rows") * columns
    )
    image_padded = pad_along(images.astype(jnp.float32), 2, half_reach)
    row_mix = slide_padded(image_padded, row_taps, 2, columns).astype(jnp.bfloat16)
    row_mix = lax.optimization_barrier(row_mix)
    mix_columns = lax.all_to_all(row_mix, "rows", split_axis=2, concat_axis=1, tiled=True)
    mix_padded = pad_along(mix_columns.astype(jnp.float32), 1, half_reach)
    col_local = slide_padded(mix_padded, col_taps, 1, mix_columns.shape[1]).astype(jnp.bfloat16)
    col_mix = lax.all_to_all(col_local, "rows", split_axis=1, concat_axis=2, tiled=True)
    col_mix = lax.optimization_barrier(col_mix)
    block_rows, grad_rows, partials = pointwise(
        col_mix.reshape(-1, channels),
        images.reshape(-1, channels),
        cotangent.reshape(-1, channels),
        norm_gain,
        norm_shift,
        up_weight,
        up_bias,
        down_weight,
        down_bias,
        layer_scale,
    )
    scale_part, down_bias_part, down_part, up_bias_part, up_part, gain_part, shift_part = partials
    block_out = block_rows.reshape(images.shape)
    grad_rows = lax.optimization_barrier(grad_rows)
    col_grad = grad_rows.reshape(images.shape)
    grad_columns = lax.all_to_all(col_grad, "rows", split_axis=2, concat_axis=1, tiled=True)
    grad_float = grad_columns.astype(jnp.float32)
    col_part = tap_sums(grad_float, mix_padded, taps_count, 1)
    row_local = slide_padded(
        pad_along(grad_float, 1, half_reach), col_taps[::-1], 1, grad_columns.shape[1]
    ).astype(jnp.bfloat16)
    row_grad = lax.all_to_all(row_local, "rows", split_axis=1, concat_axis=2, tiled=True)
    row_grad = lax.optimization_barrier(row_grad)
    row_float = row_grad.astype(jnp.float32)
    row_part = tap_sums(row_float, image_padded, taps_count, 2)
    image_grad = (
        cotangent.astype(jnp.float32)
        + slide_padded(pad_along(row_float, 2, half_reach), row_taps[::-1], 2, columns)
    ).astype(jnp.bfloat16)
    down_total, up_total = lax.psum((down_part * pixel_scale, up_part * pixel_scale), ("rows", "rep"))
    small = (row_part, col_part, scale_part, down_bias_part, up_bias_part, gain_part, shift_part)
    (
        row_total,
        col_total,
        scale_total,
        down_bias_total,
        up_bias_total,
        gain_total,
        shift_total,
    ) = exchange_sum(tuple(part * pixel_scale for part in small), ("rows", "rep"))
    return (
        block_out,
        image_grad,
        row_total,
        col_total,
        scale_total,
        down_bias_total,
        down_total,
        up_bias_total,
        up_total,
        gain_total,
        shift_total,
    )


def exchange_sum(parts, axes):
    count = 1
    for axis in axes:
        count *= lax.axis_size(axis)
    flat = jnp.concatenate([part.reshape(-1) for part in parts])
    piece = -(-flat.shape[0] // (count * 128)) * 128
    flat = jnp.pad(flat, (0, piece * count - flat.shape[0]))
    spread = lax.all_to_all(flat.reshape(count, piece), axes, 0, 0, tiled=True)
    mine = jnp.sum(spread, axis=0, keepdims=True)
    whole = lax.all_to_all(jnp.broadcast_to(mine, (count, piece)), axes, 0, 0, tiled=True)
    return split_like(whole.reshape(-1), parts)


def split_like(flat, parts):
    out = []
    at = 0
    for part in parts:
        out.append(flat[at : at + part.size].reshape(part.shape))
        at += part.size
    return tuple(out)


def solution(mesh):
    placed = (
        P(("groups", "rep"), "rows", None, None),
        P(("groups", "rep"), "rows", None, None),
        P("groups", None),
        P("groups", None),
        P("groups"),
        P("groups"),
        P("groups", None),
        P("groups"),
        P("groups", None),
        P("groups"),
        P("groups"),
    )
    return jax.shard_map(
        per_device,
        mesh=mesh,
        in_specs=placed,
        out_specs=(
            P(("groups", "rep"), "rows", None, None),
            P(("groups", "rep"), "rows", None, None),
            P("groups", None),
            P("groups", None),
            P("groups"),
            P("groups"),
            P("groups", None),
            P("groups"),
            P("groups", None),
            P("groups"),
            P("groups"),
        ),
        check_vma=False,
    )
```

```python
import math

import jax
import jax.numpy as jnp
from jax import lax
from jax.sharding import PartitionSpec as P

EPSILON = 1e-06
CUBIC_TERM = 0.044715
TANH_SCALE = 0.7978845608028654


def activate(pre_act):
    return (
        0.5
        * pre_act
        * (1.0 + jnp.tanh(TANH_SCALE * (pre_act + CUBIC_TERM * pre_act * pre_act * pre_act)))
    )


def activate_slope(pre_act):
    inner = jnp.tanh(TANH_SCALE * (pre_act + CUBIC_TERM * pre_act * pre_act * pre_act))
    return 0.5 * (1.0 + inner) + 0.5 * pre_act * (1.0 - inner * inner) * TANH_SCALE * (
        1.0 + 3.0 * CUBIC_TERM * pre_act * pre_act
    )


def pad_along(source, direction, half_reach):
    widths = [(0, 0)] * source.ndim
    widths[direction] = (half_reach, half_reach)
    return jnp.pad(source, widths)


def slide_padded(padded, taps_table, direction, length):
    shape_out = padded.shape[:direction] + (length,) + padded.shape[direction + 1 :]
    result = jnp.zeros(shape_out, jnp.float32)
    for offset in range(taps_table.shape[0]):
        result = result + taps_table[offset] * lax.slice_in_dim(
            padded, offset, offset + length, axis=direction
        )
    return result


def tap_sums(cot_field, padded, taps_count, direction):
    length = cot_field.shape[direction]
    lead_axes = tuple(range(cot_field.ndim - 1))
    return jnp.stack(
        [
            jnp.sum(
                cot_field * lax.slice_in_dim(padded, offset, offset + length, axis=direction),
                axis=lead_axes,
            )
            for offset in range(taps_count)
        ]
    )


def pointwise(
    mix_rows,
    image_rows,
    cot_rows,
    norm_gain,
    norm_shift,
    up_weight,
    up_bias,
    down_weight,
    down_bias,
    layer_scale,
):
    mix_float = mix_rows.astype(jnp.float32)
    centered = mix_float - jnp.mean(mix_float, axis=-1, keepdims=True)
    inv_dev = lax.rsqrt(jnp.mean(centered * centered, axis=-1, keepdims=True) + EPSILON)
    standardized = centered * inv_dev
    normed = (standardized * norm_gain + norm_shift).astype(jnp.bfloat16)
    pre_act = jnp.dot(normed, up_weight, preferred_element_type=jnp.float32) + up_bias
    activated = activate(pre_act).astype(jnp.bfloat16)
    branch = jnp.dot(activated, down_weight, preferred_element_type=jnp.float32) + down_bias
    cot_float = cot_rows.astype(jnp.float32)
    block_rows = (image_rows.astype(jnp.float32) + layer_scale * branch).astype(jnp.bfloat16)
    branch_cot = cot_float * layer_scale
    branch_grad = branch_cot.astype(jnp.bfloat16)
    act_cot = lax.dot_general(
        branch_grad, down_weight, (((1,), (1,)), ((), ())), preferred_element_type=jnp.float32
    )
    pre_cot = act_cot * activate_slope(pre_act)
    pre_grad = pre_cot.astype(jnp.bfloat16)
    normed_cot = lax.dot_general(
        pre_grad, up_weight, (((1,), (1,)), ((), ())), preferred_element_type=jnp.float32
    )
    scaled_cot = normed_cot * norm_gain
    grad_rows = (
        inv_dev
        * (
            scaled_cot
            - jnp.mean(scaled_cot, axis=-1, keepdims=True)
            - standardized * jnp.mean(scaled_cot * standardized, axis=-1, keepdims=True)
        )
    ).astype(jnp.bfloat16)
    partials = (
        jnp.sum(cot_float * branch, axis=0),
        jnp.sum(branch_cot, axis=0),
        lax.dot_general(
            activated, branch_grad, (((0,), (0,)), ((), ())), preferred_element_type=jnp.float32
        ),
        jnp.sum(pre_cot, axis=0),
        lax.dot_general(
            normed, pre_grad, (((0,), (0,)), ((), ())), preferred_element_type=jnp.float32
        ),
        jnp.sum(normed_cot * standardized, axis=0),
        jnp.sum(normed_cot, axis=0),
    )
    return (block_rows, grad_rows, partials)


def per_device(
    images,
    cotangent,
    row_taps,
    col_taps,
    norm_gain,
    norm_shift,
    up_weight,
    up_bias,
    down_weight,
    down_bias,
    layer_scale,
):
    tiles_here, band_rows, columns, channels = images.shape
    taps_count = row_taps.shape[0]
    half_reach = (taps_count - 1) // 2
    pixel_scale = 1.0 / math.sqrt(
        tiles_here * lax.axis_size("rep") * band_rows * lax.axis_size("rows") * columns
    )
    image_columns = lax.all_to_all(images, "rows", split_axis=2, concat_axis=1, tiled=True)
    cot_columns = lax.all_to_all(cotangent, "rows", split_axis=2, concat_axis=1, tiled=True)
    image_padded = pad_along(images.astype(jnp.float32), 2, half_reach)
    row_mix = slide_padded(image_padded, row_taps, 2, columns).astype(jnp.bfloat16)
    row_mix = lax.optimization_barrier(row_mix)
    mix_columns = lax.all_to_all(row_mix, "rows", split_axis=2, concat_axis=1, tiled=True)
    mix_padded = pad_along(mix_columns.astype(jnp.float32), 1, half_reach)
    col_mix = slide_padded(mix_padded, col_taps, 1, mix_columns.shape[1]).astype(jnp.bfloat16)
    col_mix = lax.optimization_barrier(col_mix)
    block_rows, grad_rows, partials = pointwise(
        col_mix.reshape(-1, channels),
        image_columns.reshape(-1, channels),
        cot_columns.reshape(-1, channels),
        norm_gain,
        norm_shift,
        up_weight,
        up_bias,
        down_weight,
        down_bias,
        layer_scale,
    )
    scale_part, down_bias_part, down_part, up_bias_part, up_part, gain_part, shift_part = partials
    block_out = lax.all_to_all(
        block_rows.reshape(mix_columns.shape), "rows", split_axis=1, concat_axis=2, tiled=True
    )
    grad_rows = lax.optimization_barrier(grad_rows)
    grad_float = grad_rows.reshape(mix_columns.shape).astype(jnp.float32)
    col_part = tap_sums(grad_float, mix_padded, taps_count, 1)
    row_local = slide_padded(
        pad_along(grad_float, 1, half_reach), col_taps[::-1], 1, mix_columns.shape[1]
    ).astype(jnp.bfloat16)
    row_grad = lax.all_to_all(row_local, "rows", split_axis=1, concat_axis=2, tiled=True)
    row_grad = lax.optimization_barrier(row_grad)
    row_float = row_grad.astype(jnp.float32)
    row_part = tap_sums(row_float, image_padded, taps_count, 2)
    image_grad = (
        cotangent.astype(jnp.float32)
        + slide_padded(pad_along(row_float, 2, half_reach), row_taps[::-1], 2, columns)
    ).astype(jnp.bfloat16)
    down_total, up_total = lax.psum((down_part * pixel_scale, up_part * pixel_scale), ("rows", "rep"))
    small = (row_part, col_part, scale_part, down_bias_part, up_bias_part, gain_part, shift_part)
    (
        row_total,
        col_total,
        scale_total,
        down_bias_total,
        up_bias_total,
        gain_total,
        shift_total,
    ) = exchange_sum(tuple(part * pixel_scale for part in small), ("rows", "rep"))
    return (
        block_out,
        image_grad,
        row_total,
        col_total,
        scale_total,
        down_bias_total,
        down_total,
        up_bias_total,
        up_total,
        gain_total,
        shift_total,
    )


def exchange_sum(parts, axes):
    count = 1
    for axis in axes:
        count *= lax.axis_size(axis)
    flat = jnp.concatenate([part.reshape(-1) for part in parts])
    piece = -(-flat.shape[0] // (count * 128)) * 128
    flat = jnp.pad(flat, (0, piece * count - flat.shape[0]))
    spread = lax.all_to_all(flat.reshape(count, piece), axes, 0, 0, tiled=True)
    mine = jnp.sum(spread, axis=0, keepdims=True)
    whole = lax.all_to_all(jnp.broadcast_to(mine, (count, piece)), axes, 0, 0, tiled=True)
    return split_like(whole.reshape(-1), parts)


def split_like(flat, parts):
    out = []
    at = 0
    for part in parts:
        out.append(flat[at : at + part.size].reshape(part.shape))
        at += part.size
    return tuple(out)


def solution(mesh):
    placed = (
        P(("groups", "rep"), "rows", None, None),
        P(("groups", "rep"), "rows", None, None),
        P("groups", None),
        P("groups", None),
        P("groups"),
        P("groups"),
        P("groups", None),
        P("groups"),
        P("groups", None),
        P("groups"),
        P("groups"),
    )
    return jax.shard_map(
        per_device,
        mesh=mesh,
        in_specs=placed,
        out_specs=(
            P(("groups", "rep"), "rows", None, None),
            P(("groups", "rep"), "rows", None, None),
            P("groups", None),
            P("groups", None),
            P("groups"),
            P("groups"),
            P("groups", None),
            P("groups"),
            P("groups", None),
            P("groups"),
            P("groups"),
        ),
        check_vma=False,
    )
```

```python
import math

import jax
import jax.numpy as jnp
from jax import lax
from jax.sharding import PartitionSpec as P

EPSILON = 1e-06
CUBIC_TERM = 0.044715
TANH_SCALE = 0.7978845608028654


def activate(pre_act):
    return (
        0.5
        * pre_act
        * (1.0 + jnp.tanh(TANH_SCALE * (pre_act + CUBIC_TERM * pre_act * pre_act * pre_act)))
    )


def activate_slope(pre_act):
    inner = jnp.tanh(TANH_SCALE * (pre_act + CUBIC_TERM * pre_act * pre_act * pre_act))
    return 0.5 * (1.0 + inner) + 0.5 * pre_act * (1.0 - inner * inner) * TANH_SCALE * (
        1.0 + 3.0 * CUBIC_TERM * pre_act * pre_act
    )


def pad_along(source, direction, half_reach):
    widths = [(0, 0)] * source.ndim
    widths[direction] = (half_reach, half_reach)
    return jnp.pad(source, widths)


def slide_padded(padded, taps_table, direction, length):
    shape_out = padded.shape[:direction] + (length,) + padded.shape[direction + 1 :]
    result = jnp.zeros(shape_out, jnp.float32)
    for offset in range(taps_table.shape[0]):
        result = result + taps_table[offset] * lax.slice_in_dim(
            padded, offset, offset + length, axis=direction
        ).astype(jnp.float32)
    return result


def tap_sums(cot_field, padded, taps_count, direction):
    length = cot_field.shape[direction]
    lead_axes = tuple(range(cot_field.ndim - 1))
    return jnp.stack(
        [
            jnp.sum(
                cot_field.astype(jnp.float32)
                * lax.slice_in_dim(padded, offset, offset + length, axis=direction).astype(
                    jnp.float32
                ),
                axis=lead_axes,
            )
            for offset in range(taps_count)
        ]
    )


def pointwise(
    mix_rows,
    image_rows,
    cot_rows,
    norm_gain,
    norm_shift,
    up_weight,
    up_bias,
    down_weight,
    down_bias,
    layer_scale,
):
    mix_float = mix_rows.astype(jnp.float32)
    centered = mix_float - jnp.mean(mix_float, axis=-1, keepdims=True)
    inv_dev = lax.rsqrt(jnp.mean(centered * centered, axis=-1, keepdims=True) + EPSILON)
    standardized = centered * inv_dev
    normed = (standardized * norm_gain + norm_shift).astype(jnp.bfloat16)
    pre_act = jnp.dot(normed, up_weight, preferred_element_type=jnp.float32) + up_bias
    activated = activate(pre_act).astype(jnp.bfloat16)
    branch = jnp.dot(activated, down_weight, preferred_element_type=jnp.float32) + down_bias
    cot_float = cot_rows.astype(jnp.float32)
    block_rows = (image_rows.astype(jnp.float32) + layer_scale * branch).astype(jnp.bfloat16)
    branch_cot = cot_float * layer_scale
    branch_grad = branch_cot.astype(jnp.bfloat16)
    act_cot = lax.dot_general(
        branch_grad, down_weight, (((1,), (1,)), ((), ())), preferred_element_type=jnp.float32
    )
    pre_cot = act_cot * activate_slope(pre_act)
    pre_grad = pre_cot.astype(jnp.bfloat16)
    normed_cot = lax.dot_general(
        pre_grad, up_weight, (((1,), (1,)), ((), ())), preferred_element_type=jnp.float32
    )
    scaled_cot = normed_cot * norm_gain
    grad_rows = (
        inv_dev
        * (
            scaled_cot
            - jnp.mean(scaled_cot, axis=-1, keepdims=True)
            - standardized * jnp.mean(scaled_cot * standardized, axis=-1, keepdims=True)
        )
    ).astype(jnp.bfloat16)
    partials = (
        jnp.sum(cot_float * branch, axis=0),
        jnp.sum(branch_cot, axis=0),
        lax.dot_general(
            activated, branch_grad, (((0,), (0,)), ((), ())), preferred_element_type=jnp.float32
        ),
        jnp.sum(pre_cot, axis=0),
        lax.dot_general(
            normed, pre_grad, (((0,), (0,)), ((), ())), preferred_element_type=jnp.float32
        ),
        jnp.sum(normed_cot * standardized, axis=0),
        jnp.sum(normed_cot, axis=0),
    )
    return (block_rows, grad_rows, partials)


def per_device(
    images,
    cotangent,
    row_taps,
    col_taps,
    norm_gain,
    norm_shift,
    up_weight,
    up_bias,
    down_weight,
    down_bias,
    layer_scale,
):
    tiles_here, band_rows, columns, channels = images.shape
    taps_count = row_taps.shape[0]
    half_reach = (taps_count - 1) // 2
    pixel_scale = 1.0 / math.sqrt(
        tiles_here * lax.axis_size("rep") * band_rows * lax.axis_size("rows") * columns
    )
    image_padded = pad_along(images, 2, half_reach)
    row_mix = slide_padded(image_padded, row_taps, 2, columns).astype(jnp.bfloat16)
    row_mix = lax.optimization_barrier(row_mix)
    mix_columns = lax.all_to_all(row_mix, "rows", split_axis=2, concat_axis=1, tiled=True)
    mix_padded = pad_along(mix_columns, 1, half_reach)
    col_local = slide_padded(mix_padded, col_taps, 1, mix_columns.shape[1]).astype(jnp.bfloat16)
    col_mix = lax.all_to_all(col_local, "rows", split_axis=1, concat_axis=2, tiled=True)
    col_mix = lax.optimization_barrier(col_mix)
    block_rows, grad_rows, partials = pointwise(
        col_mix.reshape(-1, channels),
        images.reshape(-1, channels),
        cotangent.reshape(-1, channels),
        norm_gain,
        norm_shift,
        up_weight,
        up_bias,
        down_weight,
        down_bias,
        layer_scale,
    )
    scale_part, down_bias_part, down_part, up_bias_part, up_part, gain_part, shift_part = partials
    block_out = block_rows.reshape(images.shape)
    grad_rows = lax.optimization_barrier(grad_rows)
    col_grad = grad_rows.reshape(images.shape)
    grad_columns = lax.all_to_all(col_grad, "rows", split_axis=2, concat_axis=1, tiled=True)
    col_part = tap_sums(grad_columns, mix_padded, taps_count, 1)
    row_local = slide_padded(
        pad_along(grad_columns, 1, half_reach), col_taps[::-1], 1, grad_columns.shape[1]
    ).astype(jnp.bfloat16)
    row_grad = lax.all_to_all(row_local, "rows", split_axis=1, concat_axis=2, tiled=True)
    row_grad = lax.optimization_barrier(row_grad)
    row_part = tap_sums(row_grad, image_padded, taps_count, 2)
    image_grad = (
        cotangent.astype(jnp.float32)
        + slide_padded(pad_along(row_grad, 2, half_reach), row_taps[::-1], 2, columns)
    ).astype(jnp.bfloat16)
    down_total, up_total = lax.psum((down_part * pixel_scale, up_part * pixel_scale), ("rows", "rep"))
    small = (row_part, col_part, scale_part, down_bias_part, up_bias_part, gain_part, shift_part)
    (
        row_total,
        col_total,
        scale_total,
        down_bias_total,
        up_bias_total,
        gain_total,
        shift_total,
    ) = exchange_sum(tuple(part * pixel_scale for part in small), ("rows", "rep"))
    return (
        block_out,
        image_grad,
        row_total,
        col_total,
        scale_total,
        down_bias_total,
        down_total,
        up_bias_total,
        up_total,
        gain_total,
        shift_total,
    )


def exchange_sum(parts, axes):
    count = 1
    for axis in axes:
        count *= lax.axis_size(axis)
    stacked = jnp.concatenate([part.reshape(-1, 128) for part in parts])
    piece = -(-stacked.shape[0] // count)
    stacked = jnp.pad(stacked, ((0, piece * count - stacked.shape[0]), (0, 0)))
    spread = lax.all_to_all(stacked.reshape(count, piece, 128), axes, 0, 0, tiled=True)
    mine = jnp.sum(spread, axis=0, keepdims=True)
    whole = lax.all_to_all(jnp.broadcast_to(mine, (count, piece, 128)), axes, 0, 0, tiled=True)
    return split_like(whole.reshape(-1), parts)


def split_like(flat, parts):
    out = []
    at = 0
    for part in parts:
        out.append(flat[at : at + part.size].reshape(part.shape))
        at += part.size
    return tuple(out)


def solution(mesh):
    placed = (
        P(("groups", "rep"), "rows", None, None),
        P(("groups", "rep"), "rows", None, None),
        P("groups", None),
        P("groups", None),
        P("groups"),
        P("groups"),
        P("groups", None),
        P("groups"),
        P("groups", None),
        P("groups"),
        P("groups"),
    )
    return jax.shard_map(
        per_device,
        mesh=mesh,
        in_specs=placed,
        out_specs=(
            P(("groups", "rep"), "rows", None, None),
            P(("groups", "rep"), "rows", None, None),
            P("groups", None),
            P("groups", None),
            P("groups"),
            P("groups"),
            P("groups", None),
            P("groups"),
            P("groups", None),
            P("groups"),
            P("groups"),
        ),
        check_vma=False,
    )
```

```python
import math

import jax
import jax.numpy as jnp
from jax import lax
from jax.sharding import PartitionSpec as P

EPSILON = 1e-06
CUBIC_TERM = 0.044715
TANH_SCALE = 0.7978845608028654


def activate(pre_act):
    return (
        0.5
        * pre_act
        * (1.0 + jnp.tanh(TANH_SCALE * (pre_act + CUBIC_TERM * pre_act * pre_act * pre_act)))
    )


def activate_slope(pre_act):
    inner = jnp.tanh(TANH_SCALE * (pre_act + CUBIC_TERM * pre_act * pre_act * pre_act))
    return 0.5 * (1.0 + inner) + 0.5 * pre_act * (1.0 - inner * inner) * TANH_SCALE * (
        1.0 + 3.0 * CUBIC_TERM * pre_act * pre_act
    )


def pad_along(source, direction, half_reach):
    widths = [(0, 0)] * source.ndim
    widths[direction] = (half_reach, half_reach)
    return jnp.pad(source, widths)


def slide_padded(padded, taps_table, direction, length):
    shape_out = padded.shape[:direction] + (length,) + padded.shape[direction + 1 :]
    result = jnp.zeros(shape_out, jnp.float32)
    for offset in range(taps_table.shape[0]):
        result = result + taps_table[offset] * lax.slice_in_dim(
            padded, offset, offset + length, axis=direction
        ).astype(jnp.float32)
    return result


def tap_sums(cot_field, padded, taps_count, direction):
    length = cot_field.shape[direction]
    lead_axes = tuple(range(cot_field.ndim - 1))
    return jnp.stack(
        [
            jnp.sum(
                cot_field.astype(jnp.float32)
                * lax.slice_in_dim(padded, offset, offset + length, axis=direction).astype(
                    jnp.float32
                ),
                axis=lead_axes,
            )
            for offset in range(taps_count)
        ]
    )


def pointwise(
    mix_rows,
    image_rows,
    cot_rows,
    norm_gain,
    norm_shift,
    up_weight,
    up_bias,
    down_weight,
    down_bias,
    layer_scale,
):
    mix_float = mix_rows.astype(jnp.float32)
    centered = mix_float - jnp.mean(mix_float, axis=-1, keepdims=True)
    inv_dev = lax.rsqrt(jnp.mean(centered * centered, axis=-1, keepdims=True) + EPSILON)
    standardized = centered * inv_dev
    normed = (standardized * norm_gain + norm_shift).astype(jnp.bfloat16)
    pre_act = jnp.dot(normed, up_weight, preferred_element_type=jnp.float32) + up_bias
    activated = activate(pre_act).astype(jnp.bfloat16)
    branch = jnp.dot(activated, down_weight, preferred_element_type=jnp.float32) + down_bias
    cot_float = cot_rows.astype(jnp.float32)
    block_rows = (image_rows.astype(jnp.float32) + layer_scale * branch).astype(jnp.bfloat16)
    branch_cot = cot_float * layer_scale
    branch_grad = branch_cot.astype(jnp.bfloat16)
    act_cot = lax.dot_general(
        branch_grad, down_weight, (((1,), (1,)), ((), ())), preferred_element_type=jnp.float32
    )
    pre_cot = act_cot * activate_slope(pre_act)
    pre_grad = pre_cot.astype(jnp.bfloat16)
    normed_cot = lax.dot_general(
        pre_grad, up_weight, (((1,), (1,)), ((), ())), preferred_element_type=jnp.float32
    )
    scaled_cot = normed_cot * norm_gain
    grad_rows = (
        inv_dev
        * (
            scaled_cot
            - jnp.mean(scaled_cot, axis=-1, keepdims=True)
            - standardized * jnp.mean(scaled_cot * standardized, axis=-1, keepdims=True)
        )
    ).astype(jnp.bfloat16)
    partials = (
        jnp.sum(cot_float * branch, axis=0),
        jnp.sum(branch_cot, axis=0),
        lax.dot_general(
            activated, branch_grad, (((0,), (0,)), ((), ())), preferred_element_type=jnp.float32
        ),
        jnp.sum(pre_cot, axis=0),
        lax.dot_general(
            normed, pre_grad, (((0,), (0,)), ((), ())), preferred_element_type=jnp.float32
        ),
        jnp.sum(normed_cot * standardized, axis=0),
        jnp.sum(normed_cot, axis=0),
    )
    return (block_rows, grad_rows, partials)


def per_device(
    images,
    cotangent,
    row_taps,
    col_taps,
    norm_gain,
    norm_shift,
    up_weight,
    up_bias,
    down_weight,
    down_bias,
    layer_scale,
):
    tiles_here, band_rows, columns, channels = images.shape
    taps_count = row_taps.shape[0]
    half_reach = (taps_count - 1) // 2
    pixel_scale = 1.0 / math.sqrt(
        tiles_here * lax.axis_size("rep") * band_rows * lax.axis_size("rows") * columns
    )
    image_padded = pad_along(images.astype(jnp.float32), 2, half_reach)
    row_mix = slide_padded(image_padded, row_taps, 2, columns).astype(jnp.bfloat16)
    row_mix = lax.optimization_barrier(row_mix)
    mix_columns = lax.all_to_all(row_mix, "rows", split_axis=2, concat_axis=1, tiled=True)
    mix_padded = pad_along(mix_columns.astype(jnp.float32), 1, half_reach)
    col_local = slide_padded(mix_padded, col_taps, 1, mix_columns.shape[1]).astype(jnp.bfloat16)
    col_mix = lax.all_to_all(col_local, "rows", split_axis=1, concat_axis=2, tiled=True)
    col_mix = lax.optimization_barrier(col_mix)
    block_rows, grad_rows, partials = pointwise(
        col_mix.reshape(-1, channels),
        images.reshape(-1, channels),
        cotangent.reshape(-1, channels),
        norm_gain,
        norm_shift,
        up_weight,
        up_bias,
        down_weight,
        down_bias,
        layer_scale,
    )
    scale_part, down_bias_part, down_part, up_bias_part, up_part, gain_part, shift_part = partials
    block_out = block_rows.reshape(images.shape)
    grad_rows = lax.optimization_barrier(grad_rows)
    col_grad = grad_rows.reshape(images.shape)
    grad_columns = lax.all_to_all(col_grad, "rows", split_axis=2, concat_axis=1, tiled=True)
    grad_float = grad_columns.astype(jnp.float32)
    col_part = tap_sums(grad_float, mix_padded, taps_count, 1)
    row_local = slide_padded(
        pad_along(grad_float, 1, half_reach), col_taps[::-1], 1, grad_columns.shape[1]
    ).astype(jnp.bfloat16)
    row_grad = lax.all_to_all(row_local, "rows", split_axis=1, concat_axis=2, tiled=True)
    row_grad = lax.optimization_barrier(row_grad)
    row_part = tap_sums(row_grad, pad_along(images, 2, half_reach), taps_count, 2)
    image_grad = (
        cotangent.astype(jnp.float32)
        + slide_padded(pad_along(row_grad, 2, half_reach), row_taps[::-1], 2, columns)
    ).astype(jnp.bfloat16)
    down_total, up_total = lax.optimization_barrier(
        lax.psum((down_part * pixel_scale, up_part * pixel_scale), ("rows", "rep"))
    )
    small = (row_part, col_part, scale_part, down_bias_part, up_bias_part, gain_part, shift_part)
    (
        row_total,
        col_total,
        scale_total,
        down_bias_total,
        up_bias_total,
        gain_total,
        shift_total,
    ) = exchange_sum(tuple(part * pixel_scale for part in small), ("rows", "rep"))
    return (
        block_out,
        image_grad,
        row_total,
        col_total,
        scale_total,
        down_bias_total,
        down_total,
        up_bias_total,
        up_total,
        gain_total,
        shift_total,
    )


def exchange_sum(parts, axes):
    count = 1
    for axis in axes:
        count *= lax.axis_size(axis)
    stacked = jnp.concatenate([part.reshape(-1, 128) for part in parts])
    piece = -(-stacked.shape[0] // count)
    stacked = jnp.pad(stacked, ((0, piece * count - stacked.shape[0]), (0, 0)))
    spread = lax.all_to_all(stacked.reshape(count, piece, 128), axes, 0, 0, tiled=True)
    mine = jnp.sum(spread, axis=0, keepdims=True)
    whole = lax.all_to_all(jnp.broadcast_to(mine, (count, piece, 128)), axes, 0, 0, tiled=True)
    return split_like(whole.reshape(-1), parts)


def split_like(flat, parts):
    out = []
    at = 0
    for part in parts:
        out.append(flat[at : at + part.size].reshape(part.shape))
        at += part.size
    return tuple(out)


def solution(mesh):
    placed = (
        P(("groups", "rep"), "rows", None, None),
        P(("groups", "rep"), "rows", None, None),
        P("groups", None),
        P("groups", None),
        P("groups"),
        P("groups"),
        P("groups", None),
        P("groups"),
        P("groups", None),
        P("groups"),
        P("groups"),
    )
    return jax.shard_map(
        per_device,
        mesh=mesh,
        in_specs=placed,
        out_specs=(
            P(("groups", "rep"), "rows", None, None),
            P(("groups", "rep"), "rows", None, None),
            P("groups", None),
            P("groups", None),
            P("groups"),
            P("groups"),
            P("groups", None),
            P("groups"),
            P("groups", None),
            P("groups"),
            P("groups"),
        ),
        check_vma=False,
    )
```

```python
import math

import jax
import jax.numpy as jnp
from jax import lax
from jax.sharding import PartitionSpec as P

EPSILON = 1e-06
CUBIC_TERM = 0.044715
TANH_SCALE = 0.7978845608028654


def activate(pre_act):
    return (
        0.5
        * pre_act
        * (1.0 + jnp.tanh(TANH_SCALE * (pre_act + CUBIC_TERM * pre_act * pre_act * pre_act)))
    )


def activate_slope(pre_act):
    inner = jnp.tanh(TANH_SCALE * (pre_act + CUBIC_TERM * pre_act * pre_act * pre_act))
    return 0.5 * (1.0 + inner) + 0.5 * pre_act * (1.0 - inner * inner) * TANH_SCALE * (
        1.0 + 3.0 * CUBIC_TERM * pre_act * pre_act
    )


def pad_along(source, direction, half_reach):
    widths = [(0, 0)] * source.ndim
    widths[direction] = (half_reach, half_reach)
    return jnp.pad(source, widths)


def slide_padded(padded, taps_table, direction, length):
    shape_out = padded.shape[:direction] + (length,) + padded.shape[direction + 1 :]
    result = jnp.zeros(shape_out, jnp.float32)
    for offset in range(taps_table.shape[0]):
        result = result + taps_table[offset] * lax.slice_in_dim(
            padded, offset, offset + length, axis=direction
        ).astype(jnp.float32)
    return result


def tap_sums(cot_field, padded, taps_count, direction):
    length = cot_field.shape[direction]
    lead_axes = tuple(range(cot_field.ndim - 1))
    return jnp.stack(
        [
            jnp.sum(
                cot_field.astype(jnp.float32)
                * lax.slice_in_dim(padded, offset, offset + length, axis=direction).astype(
                    jnp.float32
                ),
                axis=lead_axes,
            )
            for offset in range(taps_count)
        ]
    )


def pointwise(
    mix_rows,
    image_rows,
    cot_rows,
    norm_gain,
    norm_shift,
    up_weight,
    up_bias,
    down_weight,
    down_bias,
    layer_scale,
):
    mix_float = mix_rows.astype(jnp.float32)
    centered = mix_float - jnp.mean(mix_float, axis=-1, keepdims=True)
    inv_dev = lax.rsqrt(jnp.mean(centered * centered, axis=-1, keepdims=True) + EPSILON)
    standardized = centered * inv_dev
    normed = (standardized * norm_gain + norm_shift).astype(jnp.bfloat16)
    pre_act = jnp.dot(normed, up_weight, preferred_element_type=jnp.float32) + up_bias
    activated = activate(pre_act).astype(jnp.bfloat16)
    branch = jnp.dot(activated, down_weight, preferred_element_type=jnp.float32) + down_bias
    cot_float = cot_rows.astype(jnp.float32)
    block_rows = (image_rows.astype(jnp.float32) + layer_scale * branch).astype(jnp.bfloat16)
    branch_cot = cot_float * layer_scale
    branch_grad = branch_cot.astype(jnp.bfloat16)
    act_cot = lax.dot_general(
        branch_grad, down_weight, (((1,), (1,)), ((), ())), preferred_element_type=jnp.float32
    )
    pre_cot = act_cot * activate_slope(pre_act)
    pre_grad = pre_cot.astype(jnp.bfloat16)
    normed_cot = lax.dot_general(
        pre_grad, up_weight, (((1,), (1,)), ((), ())), preferred_element_type=jnp.float32
    )
    scaled_cot = normed_cot * norm_gain
    grad_rows = (
        inv_dev
        * (
            scaled_cot
            - jnp.mean(scaled_cot, axis=-1, keepdims=True)
            - standardized * jnp.mean(scaled_cot * standardized, axis=-1, keepdims=True)
        )
    ).astype(jnp.bfloat16)
    partials = (
        jnp.sum(cot_float * branch, axis=0),
        jnp.sum(branch_cot, axis=0),
        lax.dot_general(
            activated, branch_grad, (((0,), (0,)), ((), ())), preferred_element_type=jnp.float32
        ),
        jnp.sum(pre_cot, axis=0),
        lax.dot_general(
            normed, pre_grad, (((0,), (0,)), ((), ())), preferred_element_type=jnp.float32
        ),
        jnp.sum(normed_cot * standardized, axis=0),
        jnp.sum(normed_cot, axis=0),
    )
    return (block_rows, grad_rows, partials)


def per_device(
    images,
    cotangent,
    row_taps,
    col_taps,
    norm_gain,
    norm_shift,
    up_weight,
    up_bias,
    down_weight,
    down_bias,
    layer_scale,
):
    tiles_here, band_rows, columns, channels = images.shape
    taps_count = row_taps.shape[0]
    half_reach = (taps_count - 1) // 2
    pixel_scale = 1.0 / math.sqrt(
        tiles_here * lax.axis_size("rep") * band_rows * lax.axis_size("rows") * columns
    )
    image_padded = pad_along(images.astype(jnp.float32), 2, half_reach)
    row_mix = slide_padded(image_padded, row_taps, 2, columns).astype(jnp.bfloat16)
    row_mix = lax.optimization_barrier(row_mix)
    mix_columns = lax.all_to_all(row_mix, "rows", split_axis=2, concat_axis=1, tiled=True)
    mix_padded = pad_along(mix_columns.astype(jnp.float32), 1, half_reach)
    col_local = slide_padded(mix_padded, col_taps, 1, mix_columns.shape[1]).astype(jnp.bfloat16)
    col_mix = lax.all_to_all(col_local, "rows", split_axis=1, concat_axis=2, tiled=True)
    col_mix = lax.optimization_barrier(col_mix)
    block_rows, grad_rows, partials = pointwise(
        col_mix.reshape(-1, channels),
        images.reshape(-1, channels),
        cotangent.reshape(-1, channels),
        norm_gain,
        norm_shift,
        up_weight,
        up_bias,
        down_weight,
        down_bias,
        layer_scale,
    )
    scale_part, down_bias_part, down_part, up_bias_part, up_part, gain_part, shift_part = partials
    block_out = block_rows.reshape(images.shape)
    grad_rows = lax.optimization_barrier(grad_rows)
    col_grad = grad_rows.reshape(images.shape)
    grad_columns = lax.all_to_all(col_grad, "rows", split_axis=2, concat_axis=1, tiled=True)
    grad_float = grad_columns.astype(jnp.float32)
    col_part = tap_sums(grad_float, mix_padded, taps_count, 1)
    row_local = slide_padded(
        pad_along(grad_float, 1, half_reach), col_taps[::-1], 1, grad_columns.shape[1]
    ).astype(jnp.bfloat16)
    row_grad = lax.all_to_all(row_local, "rows", split_axis=1, concat_axis=2, tiled=True)
    row_grad = lax.optimization_barrier(row_grad)
    row_part = tap_sums(row_grad, pad_along(images, 2, half_reach), taps_count, 2)
    image_grad = (
        cotangent.astype(jnp.float32)
        + slide_padded(pad_along(row_grad, 2, half_reach), row_taps[::-1], 2, columns)
    ).astype(jnp.bfloat16)
    down_total, up_total = lax.optimization_barrier(
        lax.psum((down_part * pixel_scale, up_part * pixel_scale), ("rows", "rep"))
    )
    small = (row_part, col_part, scale_part, down_bias_part, up_bias_part, gain_part, shift_part)
    small, image_grad = lax.optimization_barrier((small, image_grad))
    (
        row_total,
        col_total,
        scale_total,
        down_bias_total,
        up_bias_total,
        gain_total,
        shift_total,
    ) = exchange_sum(tuple(part * pixel_scale for part in small), ("rows", "rep"))
    return (
        block_out,
        image_grad,
        row_total,
        col_total,
        scale_total,
        down_bias_total,
        down_total,
        up_bias_total,
        up_total,
        gain_total,
        shift_total,
    )


def exchange_sum(parts, axes):
    count = 1
    for axis in axes:
        count *= lax.axis_size(axis)
    stacked = jnp.concatenate([part.reshape(-1, 128) for part in parts])
    piece = -(-stacked.shape[0] // count)
    stacked = jnp.pad(stacked, ((0, piece * count - stacked.shape[0]), (0, 0)))
    spread = lax.all_to_all(stacked.reshape(count, piece, 128), axes, 0, 0, tiled=True)
    mine = jnp.sum(spread, axis=0, keepdims=True)
    whole = lax.all_to_all(jnp.broadcast_to(mine, (count, piece, 128)), axes, 0, 0, tiled=True)
    return split_like(whole.reshape(-1), parts)


def split_like(flat, parts):
    out = []
    at = 0
    for part in parts:
        out.append(flat[at : at + part.size].reshape(part.shape))
        at += part.size
    return tuple(out)


def solution(mesh):
    placed = (
        P(("groups", "rep"), "rows", None, None),
        P(("groups", "rep"), "rows", None, None),
        P("groups", None),
        P("groups", None),
        P("groups"),
        P("groups"),
        P("groups", None),
        P("groups"),
        P("groups", None),
        P("groups"),
        P("groups"),
    )
    return jax.shard_map(
        per_device,
        mesh=mesh,
        in_specs=placed,
        out_specs=(
            P(("groups", "rep"), "rows", None, None),
            P(("groups", "rep"), "rows", None, None),
            P("groups", None),
            P("groups", None),
            P("groups"),
            P("groups"),
            P("groups", None),
            P("groups"),
            P("groups", None),
            P("groups"),
            P("groups"),
        ),
        check_vma=False,
    )
```

```python
import math

import jax
import jax.numpy as jnp
from jax import lax
from jax.sharding import PartitionSpec as P

EPSILON = 1e-06
CUBIC_TERM = 0.044715
TANH_SCALE = 0.7978845608028654


def activate(pre_act):
    return (
        0.5
        * pre_act
        * (1.0 + jnp.tanh(TANH_SCALE * (pre_act + CUBIC_TERM * pre_act * pre_act * pre_act)))
    )


def activate_slope(pre_act):
    inner = jnp.tanh(TANH_SCALE * (pre_act + CUBIC_TERM * pre_act * pre_act * pre_act))
    return 0.5 * (1.0 + inner) + 0.5 * pre_act * (1.0 - inner * inner) * TANH_SCALE * (
        1.0 + 3.0 * CUBIC_TERM * pre_act * pre_act
    )


def pad_along(source, direction, half_reach):
    widths = [(0, 0)] * source.ndim
    widths[direction] = (half_reach, half_reach)
    return jnp.pad(source, widths)


def slide_padded(padded, taps_table, direction, length):
    shape_out = padded.shape[:direction] + (length,) + padded.shape[direction + 1 :]
    result = jnp.zeros(shape_out, jnp.float32)
    for offset in range(taps_table.shape[0]):
        result = result + taps_table[offset] * lax.slice_in_dim(
            padded, offset, offset + length, axis=direction
        ).astype(jnp.float32)
    return result


def tap_sums(cot_field, padded, taps_count, direction):
    length = cot_field.shape[direction]
    lead_axes = tuple(range(cot_field.ndim - 1))
    return jnp.stack(
        [
            jnp.sum(
                cot_field.astype(jnp.float32)
                * lax.slice_in_dim(padded, offset, offset + length, axis=direction).astype(
                    jnp.float32
                ),
                axis=lead_axes,
            )
            for offset in range(taps_count)
        ]
    )


def pointwise(
    mix_rows,
    image_rows,
    cot_rows,
    norm_gain,
    norm_shift,
    up_weight,
    up_bias,
    down_weight,
    down_bias,
    layer_scale,
):
    mix_float = mix_rows.astype(jnp.float32)
    centered = mix_float - jnp.mean(mix_float, axis=-1, keepdims=True)
    inv_dev = lax.rsqrt(jnp.mean(centered * centered, axis=-1, keepdims=True) + EPSILON)
    standardized = centered * inv_dev
    normed = (standardized * norm_gain + norm_shift).astype(jnp.bfloat16)
    pre_act = jnp.dot(normed, up_weight, preferred_element_type=jnp.float32) + up_bias
    activated = activate(pre_act).astype(jnp.bfloat16)
    branch = jnp.dot(activated, down_weight, preferred_element_type=jnp.float32) + down_bias
    cot_float = cot_rows.astype(jnp.float32)
    block_rows = (image_rows.astype(jnp.float32) + layer_scale * branch).astype(jnp.bfloat16)
    branch_cot = cot_float * layer_scale
    branch_grad = branch_cot.astype(jnp.bfloat16)
    act_cot = lax.dot_general(
        branch_grad, down_weight, (((1,), (1,)), ((), ())), preferred_element_type=jnp.float32
    )
    pre_cot = act_cot * activate_slope(pre_act)
    pre_grad = pre_cot.astype(jnp.bfloat16)
    normed_cot = lax.dot_general(
        pre_grad, up_weight, (((1,), (1,)), ((), ())), preferred_element_type=jnp.float32
    )
    scaled_cot = normed_cot * norm_gain
    grad_rows = (
        inv_dev
        * (
            scaled_cot
            - jnp.mean(scaled_cot, axis=-1, keepdims=True)
            - standardized * jnp.mean(scaled_cot * standardized, axis=-1, keepdims=True)
        )
    ).astype(jnp.bfloat16)
    partials = (
        jnp.sum(cot_float * branch, axis=0),
        jnp.sum(branch_cot, axis=0),
        lax.dot_general(
            activated, branch_grad, (((0,), (0,)), ((), ())), preferred_element_type=jnp.float32
        ),
        jnp.sum(pre_cot, axis=0),
        lax.dot_general(
            normed, pre_grad, (((0,), (0,)), ((), ())), preferred_element_type=jnp.float32
        ),
        jnp.sum(normed_cot * standardized, axis=0),
        jnp.sum(normed_cot, axis=0),
    )
    return (block_rows, grad_rows, partials)


def per_device(
    images,
    cotangent,
    row_taps,
    col_taps,
    norm_gain,
    norm_shift,
    up_weight,
    up_bias,
    down_weight,
    down_bias,
    layer_scale,
):
    tiles_here, band_rows, columns, channels = images.shape
    taps_count = row_taps.shape[0]
    half_reach = (taps_count - 1) // 2
    pixel_scale = 1.0 / math.sqrt(
        tiles_here * lax.axis_size("rep") * band_rows * lax.axis_size("rows") * columns
    )
    image_padded = pad_along(images.astype(jnp.float32), 2, half_reach)
    row_mix = slide_padded(image_padded, row_taps, 2, columns).astype(jnp.bfloat16)
    row_mix = lax.optimization_barrier(row_mix)
    mix_columns = lax.all_to_all(row_mix, "rows", split_axis=2, concat_axis=1, tiled=True)
    mix_padded = pad_along(mix_columns.astype(jnp.float32), 1, half_reach)
    col_local = slide_padded(mix_padded, col_taps, 1, mix_columns.shape[1]).astype(jnp.bfloat16)
    col_mix = lax.all_to_all(col_local, "rows", split_axis=1, concat_axis=2, tiled=True)
    col_mix = lax.optimization_barrier(col_mix)
    block_rows, grad_rows, partials = pointwise(
        col_mix.reshape(-1, channels),
        images.reshape(-1, channels),
        cotangent.reshape(-1, channels),
        norm_gain,
        norm_shift,
        up_weight,
        up_bias,
        down_weight,
        down_bias,
        layer_scale,
    )
    scale_part, down_bias_part, down_part, up_bias_part, up_part, gain_part, shift_part = partials
    block_out = block_rows.reshape(images.shape)
    grad_rows = lax.optimization_barrier(grad_rows)
    col_grad = grad_rows.reshape(images.shape)
    grad_columns = lax.all_to_all(col_grad, "rows", split_axis=2, concat_axis=1, tiled=True)
    grad_float = grad_columns.astype(jnp.float32)
    col_part = tap_sums(grad_float, mix_padded, taps_count, 1)
    row_local = slide_padded(
        pad_along(grad_float, 1, half_reach), col_taps[::-1], 1, grad_columns.shape[1]
    ).astype(jnp.bfloat16)
    row_grad = lax.all_to_all(row_local, "rows", split_axis=1, concat_axis=2, tiled=True)
    row_grad = lax.optimization_barrier(row_grad)
    row_part = tap_sums(row_grad, pad_along(images, 2, half_reach), taps_count, 2)
    row_part, row_grad = lax.optimization_barrier((row_part, row_grad))
    image_grad = (
        cotangent.astype(jnp.float32)
        + slide_padded(pad_along(row_grad, 2, half_reach), row_taps[::-1], 2, columns)
    ).astype(jnp.bfloat16)
    down_total, up_total = lax.optimization_barrier(
        lax.psum((down_part * pixel_scale, up_part * pixel_scale), ("rows", "rep"))
    )
    small = (row_part, col_part, scale_part, down_bias_part, up_bias_part, gain_part, shift_part)
    (
        row_total,
        col_total,
        scale_total,
        down_bias_total,
        up_bias_total,
        gain_total,
        shift_total,
    ), image_grad = exchange_sum(tuple(part * pixel_scale for part in small), ("rows", "rep"), image_grad)
    return (
        block_out,
        image_grad,
        row_total,
        col_total,
        scale_total,
        down_bias_total,
        down_total,
        up_bias_total,
        up_total,
        gain_total,
        shift_total,
    )


def exchange_sum(parts, axes, companion):
    count = 1
    for axis in axes:
        count *= lax.axis_size(axis)
    stacked = jnp.concatenate([part.reshape(-1, 128) for part in parts])
    piece = -(-stacked.shape[0] // count)
    stacked = jnp.pad(stacked, ((0, piece * count - stacked.shape[0]), (0, 0)))
    spread = lax.all_to_all(stacked.reshape(count, piece, 128), axes, 0, 0, tiled=True)
    mine = jnp.sum(spread, axis=0, keepdims=True)
    mine, companion = lax.optimization_barrier((mine, companion))
    whole = lax.all_to_all(jnp.broadcast_to(mine, (count, piece, 128)), axes, 0, 0, tiled=True)
    return split_like(whole.reshape(-1), parts), companion


def split_like(flat, parts):
    out = []
    at = 0
    for part in parts:
        out.append(flat[at : at + part.size].reshape(part.shape))
        at += part.size
    return tuple(out)


def solution(mesh):
    placed = (
        P(("groups", "rep"), "rows", None, None),
        P(("groups", "rep"), "rows", None, None),
        P("groups", None),
        P("groups", None),
        P("groups"),
        P("groups"),
        P("groups", None),
        P("groups"),
        P("groups", None),
        P("groups"),
        P("groups"),
    )
    return jax.shard_map(
        per_device,
        mesh=mesh,
        in_specs=placed,
        out_specs=(
            P(("groups", "rep"), "rows", None, None),
            P(("groups", "rep"), "rows", None, None),
            P("groups", None),
            P("groups", None),
            P("groups"),
            P("groups"),
            P("groups", None),
            P("groups"),
            P("groups", None),
            P("groups"),
            P("groups"),
        ),
        check_vma=False,
    )
```

```python
import math

import jax
import jax.numpy as jnp
from jax import lax
from jax.sharding import PartitionSpec as P

EPSILON = 1e-06
CUBIC_TERM = 0.044715
TANH_SCALE = 0.7978845608028654


def activate(pre_act):
    return (
        0.5
        * pre_act
        * (1.0 + jnp.tanh(TANH_SCALE * (pre_act + CUBIC_TERM * pre_act * pre_act * pre_act)))
    )


def activate_slope(pre_act):
    inner = jnp.tanh(TANH_SCALE * (pre_act + CUBIC_TERM * pre_act * pre_act * pre_act))
    return 0.5 * (1.0 + inner) + 0.5 * pre_act * (1.0 - inner * inner) * TANH_SCALE * (
        1.0 + 3.0 * CUBIC_TERM * pre_act * pre_act
    )


def pad_along(source, direction, half_reach):
    widths = [(0, 0)] * source.ndim
    widths[direction] = (half_reach, half_reach)
    return jnp.pad(source, widths)


def slide_padded(padded, taps_table, direction, length):
    shape_out = padded.shape[:direction] + (length,) + padded.shape[direction + 1 :]
    result = jnp.zeros(shape_out, jnp.float32)
    for offset in range(taps_table.shape[0]):
        result = result + taps_table[offset] * lax.slice_in_dim(
            padded, offset, offset + length, axis=direction
        ).astype(jnp.float32)
    return result


def tap_sums(cot_field, padded, taps_count, direction):
    length = cot_field.shape[direction]
    lead_axes = tuple(range(cot_field.ndim - 1))
    return jnp.stack(
        [
            jnp.sum(
                cot_field.astype(jnp.float32)
                * lax.slice_in_dim(padded, offset, offset + length, axis=direction).astype(
                    jnp.float32
                ),
                axis=lead_axes,
            )
            for offset in range(taps_count)
        ]
    )


def pointwise(
    mix_rows,
    image_rows,
    cot_rows,
    norm_gain,
    norm_shift,
    up_weight,
    up_bias,
    down_weight,
    down_bias,
    layer_scale,
):
    mix_float = mix_rows.astype(jnp.float32)
    centered = mix_float - jnp.mean(mix_float, axis=-1, keepdims=True)
    inv_dev = lax.rsqrt(jnp.mean(centered * centered, axis=-1, keepdims=True) + EPSILON)
    standardized = centered * inv_dev
    normed = (standardized * norm_gain + norm_shift).astype(jnp.bfloat16)
    pre_act = jnp.dot(normed, up_weight, preferred_element_type=jnp.float32) + up_bias
    activated = activate(pre_act).astype(jnp.bfloat16)
    branch = jnp.dot(activated, down_weight, preferred_element_type=jnp.float32) + down_bias
    cot_float = cot_rows.astype(jnp.float32)
    block_rows = (image_rows.astype(jnp.float32) + layer_scale * branch).astype(jnp.bfloat16)
    branch_cot = cot_float * layer_scale
    branch_grad = branch_cot.astype(jnp.bfloat16)
    act_cot = lax.dot_general(
        branch_grad, down_weight, (((1,), (1,)), ((), ())), preferred_element_type=jnp.float32
    )
    pre_cot = act_cot * activate_slope(pre_act)
    pre_grad = pre_cot.astype(jnp.bfloat16)
    normed_cot = lax.dot_general(
        pre_grad, up_weight, (((1,), (1,)), ((), ())), preferred_element_type=jnp.float32
    )
    scaled_cot = normed_cot * norm_gain
    grad_rows = (
        inv_dev
        * (
            scaled_cot
            - jnp.mean(scaled_cot, axis=-1, keepdims=True)
            - standardized * jnp.mean(scaled_cot * standardized, axis=-1, keepdims=True)
        )
    ).astype(jnp.bfloat16)
    partials = (
        jnp.sum(cot_float * branch, axis=0),
        jnp.sum(branch_cot, axis=0),
        lax.dot_general(
            activated, branch_grad, (((0,), (0,)), ((), ())), preferred_element_type=jnp.float32
        ),
        jnp.sum(pre_cot, axis=0),
        lax.dot_general(
            normed, pre_grad, (((0,), (0,)), ((), ())), preferred_element_type=jnp.float32
        ),
        jnp.sum(normed_cot * standardized, axis=0),
        jnp.sum(normed_cot, axis=0),
    )
    return (block_rows, grad_rows, partials)


def per_device(
    images,
    cotangent,
    row_taps,
    col_taps,
    norm_gain,
    norm_shift,
    up_weight,
    up_bias,
    down_weight,
    down_bias,
    layer_scale,
):
    tiles_here, band_rows, columns, channels = images.shape
    taps_count = row_taps.shape[0]
    half_reach = (taps_count - 1) // 2
    pixel_scale = 1.0 / math.sqrt(
        tiles_here * lax.axis_size("rep") * band_rows * lax.axis_size("rows") * columns
    )
    halves = 2 if channels % 256 == 0 else 1
    width = channels // halves
    mix_parts = []
    col_parts = []
    for half in range(halves):
        lanes = slice(half * width, (half + 1) * width)
        image_padded = pad_along(images[..., lanes].astype(jnp.float32), 2, half_reach)
        row_mix = slide_padded(image_padded, row_taps[:, lanes], 2, columns).astype(jnp.bfloat16)
        row_mix = lax.optimization_barrier(row_mix)
        mix_columns = lax.all_to_all(row_mix, "rows", split_axis=2, concat_axis=1, tiled=True)
        mix_padded = pad_along(mix_columns.astype(jnp.float32), 1, half_reach)
        col_local = slide_padded(
            mix_padded, col_taps[:, lanes], 1, mix_columns.shape[1]
        ).astype(jnp.bfloat16)
        col_parts.append(lax.all_to_all(col_local, "rows", split_axis=1, concat_axis=2, tiled=True))
        mix_parts.append(mix_padded)
    col_mix = lax.optimization_barrier(jnp.concatenate(col_parts, axis=-1))
    block_rows, grad_rows, partials = pointwise(
        col_mix.reshape(-1, channels),
        images.reshape(-1, channels),
        cotangent.reshape(-1, channels),
        norm_gain,
        norm_shift,
        up_weight,
        up_bias,
        down_weight,
        down_bias,
        layer_scale,
    )
    scale_part, down_bias_part, down_part, up_bias_part, up_part, gain_part, shift_part = partials
    block_out = block_rows.reshape(images.shape)
    grad_rows = lax.optimization_barrier(grad_rows)
    col_grad = grad_rows.reshape(images.shape)
    grad_columns = lax.all_to_all(col_grad, "rows", split_axis=2, concat_axis=1, tiled=True)
    grad_float = grad_columns.astype(jnp.float32)
    col_part = jnp.concatenate(
        [
            tap_sums(grad_float[..., half * width : (half + 1) * width], mix_parts[half], taps_count, 1)
            for half in range(halves)
        ],
        axis=-1,
    )
    row_local = slide_padded(
        pad_along(grad_float, 1, half_reach), col_taps[::-1], 1, grad_columns.shape[1]
    ).astype(jnp.bfloat16)
    row_grad = lax.all_to_all(row_local, "rows", split_axis=1, concat_axis=2, tiled=True)
    row_grad = lax.optimization_barrier(row_grad)
    row_part = tap_sums(row_grad, pad_along(images, 2, half_reach), taps_count, 2)
    row_part, row_grad = lax.optimization_barrier((row_part, row_grad))
    image_grad = (
        cotangent.astype(jnp.float32)
        + slide_padded(pad_along(row_grad, 2, half_reach), row_taps[::-1], 2, columns)
    ).astype(jnp.bfloat16)
    down_total, up_total = lax.optimization_barrier(
        lax.psum((down_part * pixel_scale, up_part * pixel_scale), ("rows", "rep"))
    )
    small = (row_part, col_part, scale_part, down_bias_part, up_bias_part, gain_part, shift_part)
    (
        row_total,
        col_total,
        scale_total,
        down_bias_total,
        up_bias_total,
        gain_total,
        shift_total,
    ), image_grad = exchange_sum(tuple(part * pixel_scale for part in small), ("rows", "rep"), image_grad)
    return (
        block_out,
        image_grad,
        row_total,
        col_total,
        scale_total,
        down_bias_total,
        down_total,
        up_bias_total,
        up_total,
        gain_total,
        shift_total,
    )


def exchange_sum(parts, axes, companion):
    count = 1
    for axis in axes:
        count *= lax.axis_size(axis)
    stacked = jnp.concatenate([part.reshape(-1, 128) for part in parts])
    piece = -(-stacked.shape[0] // count)
    stacked = jnp.pad(stacked, ((0, piece * count - stacked.shape[0]), (0, 0)))
    spread = lax.all_to_all(stacked.reshape(count, piece, 128), axes, 0, 0, tiled=True)
    mine = jnp.sum(spread, axis=0, keepdims=True)
    mine, companion = lax.optimization_barrier((mine, companion))
    whole = lax.all_to_all(jnp.broadcast_to(mine, (count, piece, 128)), axes, 0, 0, tiled=True)
    return split_like(whole.reshape(-1), parts), companion


def split_like(flat, parts):
    out = []
    at = 0
    for part in parts:
        out.append(flat[at : at + part.size].reshape(part.shape))
        at += part.size
    return tuple(out)


def solution(mesh):
    placed = (
        P(("groups", "rep"), "rows", None, None),
        P(("groups", "rep"), "rows", None, None),
        P("groups", None),
        P("groups", None),
        P("groups"),
        P("groups"),
        P("groups", None),
        P("groups"),
        P("groups", None),
        P("groups"),
        P("groups"),
    )
    return jax.shard_map(
        per_device,
        mesh=mesh,
        in_specs=placed,
        out_specs=(
            P(("groups", "rep"), "rows", None, None),
            P(("groups", "rep"), "rows", None, None),
            P("groups", None),
            P("groups", None),
            P("groups"),
            P("groups"),
            P("groups", None),
            P("groups"),
            P("groups", None),
            P("groups"),
            P("groups"),
        ),
        check_vma=False,
    )
```

```python
import math

import jax
import jax.numpy as jnp
from jax import lax
from jax.sharding import PartitionSpec as P

EPSILON = 1e-06
CUBIC_TERM = 0.044715
TANH_SCALE = 0.7978845608028654


def activate(pre_act):
    return (
        0.5
        * pre_act
        * (1.0 + jnp.tanh(TANH_SCALE * (pre_act + CUBIC_TERM * pre_act * pre_act * pre_act)))
    )


def activate_slope(pre_act):
    inner = jnp.tanh(TANH_SCALE * (pre_act + CUBIC_TERM * pre_act * pre_act * pre_act))
    return 0.5 * (1.0 + inner) + 0.5 * pre_act * (1.0 - inner * inner) * TANH_SCALE * (
        1.0 + 3.0 * CUBIC_TERM * pre_act * pre_act
    )


def pad_along(source, direction, half_reach):
    widths = [(0, 0)] * source.ndim
    widths[direction] = (half_reach, half_reach)
    return jnp.pad(source, widths)


def slide_padded(padded, taps_table, direction, length):
    shape_out = padded.shape[:direction] + (length,) + padded.shape[direction + 1 :]
    result = jnp.zeros(shape_out, jnp.float32)
    for offset in range(taps_table.shape[0]):
        result = result + taps_table[offset] * lax.slice_in_dim(
            padded, offset, offset + length, axis=direction
        ).astype(jnp.float32)
    return result


def tap_sums(cot_field, padded, taps_count, direction):
    length = cot_field.shape[direction]
    lead_axes = tuple(range(cot_field.ndim - 1))
    return jnp.stack(
        [
            jnp.sum(
                cot_field.astype(jnp.float32)
                * lax.slice_in_dim(padded, offset, offset + length, axis=direction).astype(
                    jnp.float32
                ),
                axis=lead_axes,
            )
            for offset in range(taps_count)
        ]
    )


def pointwise(
    mix_rows,
    image_rows,
    cot_rows,
    norm_gain,
    norm_shift,
    up_weight,
    up_bias,
    down_weight,
    down_bias,
    layer_scale,
):
    mix_float = mix_rows.astype(jnp.float32)
    centered = mix_float - jnp.mean(mix_float, axis=-1, keepdims=True)
    inv_dev = lax.rsqrt(jnp.mean(centered * centered, axis=-1, keepdims=True) + EPSILON)
    standardized = centered * inv_dev
    normed = (standardized * norm_gain + norm_shift).astype(jnp.bfloat16)
    pre_act = jnp.dot(normed, up_weight, preferred_element_type=jnp.float32) + up_bias
    activated = activate(pre_act).astype(jnp.bfloat16)
    branch = jnp.dot(activated, down_weight, preferred_element_type=jnp.float32) + down_bias
    cot_float = cot_rows.astype(jnp.float32)
    block_rows = (image_rows.astype(jnp.float32) + layer_scale * branch).astype(jnp.bfloat16)
    branch_cot = cot_float * layer_scale
    branch_grad = branch_cot.astype(jnp.bfloat16)
    act_cot = lax.dot_general(
        branch_grad, down_weight, (((1,), (1,)), ((), ())), preferred_element_type=jnp.float32
    )
    pre_cot = act_cot * activate_slope(pre_act)
    pre_grad = pre_cot.astype(jnp.bfloat16)
    normed_cot = lax.dot_general(
        pre_grad, up_weight, (((1,), (1,)), ((), ())), preferred_element_type=jnp.float32
    )
    scaled_cot = normed_cot * norm_gain
    grad_rows = (
        inv_dev
        * (
            scaled_cot
            - jnp.mean(scaled_cot, axis=-1, keepdims=True)
            - standardized * jnp.mean(scaled_cot * standardized, axis=-1, keepdims=True)
        )
    ).astype(jnp.bfloat16)
    partials = (
        jnp.sum(cot_float * branch, axis=0),
        jnp.sum(branch_cot, axis=0),
        lax.dot_general(
            activated, branch_grad, (((0,), (0,)), ((), ())), preferred_element_type=jnp.float32
        ),
        jnp.sum(pre_cot, axis=0),
        lax.dot_general(
            normed, pre_grad, (((0,), (0,)), ((), ())), preferred_element_type=jnp.float32
        ),
        jnp.sum(normed_cot * standardized, axis=0),
        jnp.sum(normed_cot, axis=0),
    )
    return (block_rows, grad_rows, partials)


def to_columns(band):
    count = lax.axis_size("rows")
    tiles, rows, width, chans = band.shape
    split = band.reshape(tiles, rows, count, width // count, chans).transpose(2, 0, 1, 3, 4)
    split = lax.all_to_all(split, "rows", 0, 0, tiled=True)
    return split.transpose(1, 0, 2, 3, 4).reshape(tiles, count * rows, width // count, chans)


def per_device(
    images,
    cotangent,
    row_taps,
    col_taps,
    norm_gain,
    norm_shift,
    up_weight,
    up_bias,
    down_weight,
    down_bias,
    layer_scale,
):
    tiles_here, band_rows, columns, channels = images.shape
    taps_count = row_taps.shape[0]
    half_reach = (taps_count - 1) // 2
    pixel_scale = 1.0 / math.sqrt(
        tiles_here * lax.axis_size("rep") * band_rows * lax.axis_size("rows") * columns
    )
    image_padded = pad_along(images.astype(jnp.float32), 2, half_reach)
    row_mix = slide_padded(image_padded, row_taps, 2, columns).astype(jnp.bfloat16)
    row_mix = lax.optimization_barrier(row_mix)
    mix_columns = to_columns(row_mix)
    mix_padded = pad_along(mix_columns.astype(jnp.float32), 1, half_reach)
    col_local = slide_padded(mix_padded, col_taps, 1, mix_columns.shape[1]).astype(jnp.bfloat16)
    col_mix = lax.all_to_all(col_local, "rows", split_axis=1, concat_axis=2, tiled=True)
    col_mix = lax.optimization_barrier(col_mix)
    block_rows, grad_rows, partials = pointwise(
        col_mix.reshape(-1, channels),
        images.reshape(-1, channels),
        cotangent.reshape(-1, channels),
        norm_gain,
        norm_shift,
        up_weight,
        up_bias,
        down_weight,
        down_bias,
        layer_scale,
    )
    scale_part, down_bias_part, down_part, up_bias_part, up_part, gain_part, shift_part = partials
    block_out = block_rows.reshape(images.shape)
    grad_rows = lax.optimization_barrier(grad_rows)
    col_grad = grad_rows.reshape(images.shape)
    grad_columns = to_columns(col_grad)
    grad_float = grad_columns.astype(jnp.float32)
    col_part = tap_sums(grad_float, mix_padded, taps_count, 1)
    row_local = slide_padded(
        pad_along(grad_float, 1, half_reach), col_taps[::-1], 1, grad_columns.shape[1]
    ).astype(jnp.bfloat16)
    row_grad = lax.all_to_all(row_local, "rows", split_axis=1, concat_axis=2, tiled=True)
    row_grad = lax.optimization_barrier(row_grad)
    row_part = tap_sums(row_grad, pad_along(images, 2, half_reach), taps_count, 2)
    row_part, row_grad = lax.optimization_barrier((row_part, row_grad))
    image_grad = (
        cotangent.astype(jnp.float32)
        + slide_padded(pad_along(row_grad, 2, half_reach), row_taps[::-1], 2, columns)
    ).astype(jnp.bfloat16)
    down_total, up_total = lax.optimization_barrier(
        lax.psum((down_part * pixel_scale, up_part * pixel_scale), ("rows", "rep"))
    )
    small = (row_part, col_part, scale_part, down_bias_part, up_bias_part, gain_part, shift_part)
    (
        row_total,
        col_total,
        scale_total,
        down_bias_total,
        up_bias_total,
        gain_total,
        shift_total,
    ), image_grad = exchange_sum(tuple(part * pixel_scale for part in small), ("rows", "rep"), image_grad)
    return (
        block_out,
        image_grad,
        row_total,
        col_total,
        scale_total,
        down_bias_total,
        down_total,
        up_bias_total,
        up_total,
        gain_total,
        shift_total,
    )


def exchange_sum(parts, axes, companion):
    count = 1
    for axis in axes:
        count *= lax.axis_size(axis)
    stacked = jnp.concatenate([part.reshape(-1, 128) for part in parts])
    piece = -(-stacked.shape[0] // count)
    stacked = jnp.pad(stacked, ((0, piece * count - stacked.shape[0]), (0, 0)))
    spread = lax.all_to_all(stacked.reshape(count, piece, 128), axes, 0, 0, tiled=True)
    mine = jnp.sum(spread, axis=0, keepdims=True)
    mine, companion = lax.optimization_barrier((mine, companion))
    whole = lax.all_to_all(jnp.broadcast_to(mine, (count, piece, 128)), axes, 0, 0, tiled=True)
    return split_like(whole.reshape(-1), parts), companion


def split_like(flat, parts):
    out = []
    at = 0
    for part in parts:
        out.append(flat[at : at + part.size].reshape(part.shape))
        at += part.size
    return tuple(out)


def solution(mesh):
    placed = (
        P(("groups", "rep"), "rows", None, None),
        P(("groups", "rep"), "rows", None, None),
        P("groups", None),
        P("groups", None),
        P("groups"),
        P("groups"),
        P("groups", None),
        P("groups"),
        P("groups", None),
        P("groups"),
        P("groups"),
    )
    return jax.shard_map(
        per_device,
        mesh=mesh,
        in_specs=placed,
        out_specs=(
            P(("groups", "rep"), "rows", None, None),
            P(("groups", "rep"), "rows", None, None),
            P("groups", None),
            P("groups", None),
            P("groups"),
            P("groups"),
            P("groups", None),
            P("groups"),
            P("groups", None),
            P("groups"),
            P("groups"),
        ),
        check_vma=False,
    )
```

```python
import math

import jax
import jax.numpy as jnp
from jax import lax
from jax.sharding import PartitionSpec as P

EPSILON = 1e-06
CUBIC_TERM = 0.044715
TANH_SCALE = 0.7978845608028654


def activate(pre_act):
    return (
        0.5
        * pre_act
        * (1.0 + jnp.tanh(TANH_SCALE * (pre_act + CUBIC_TERM * pre_act * pre_act * pre_act)))
    )


def activate_slope(pre_act):
    inner = jnp.tanh(TANH_SCALE * (pre_act + CUBIC_TERM * pre_act * pre_act * pre_act))
    return 0.5 * (1.0 + inner) + 0.5 * pre_act * (1.0 - inner * inner) * TANH_SCALE * (
        1.0 + 3.0 * CUBIC_TERM * pre_act * pre_act
    )


def pad_along(source, direction, half_reach):
    widths = [(0, 0)] * source.ndim
    widths[direction] = (half_reach, half_reach)
    return jnp.pad(source, widths)


def slide_padded(padded, taps_table, direction, length):
    shape_out = padded.shape[:direction] + (length,) + padded.shape[direction + 1 :]
    result = jnp.zeros(shape_out, jnp.float32)
    for offset in range(taps_table.shape[0]):
        result = result + taps_table[offset] * lax.slice_in_dim(
            padded, offset, offset + length, axis=direction
        ).astype(jnp.float32)
    return result


def tap_sums(cot_field, padded, taps_count, direction):
    length = cot_field.shape[direction]
    lead_axes = tuple(range(cot_field.ndim - 1))
    return jnp.stack(
        [
            jnp.sum(
                cot_field.astype(jnp.float32)
                * lax.slice_in_dim(padded, offset, offset + length, axis=direction).astype(
                    jnp.float32
                ),
                axis=lead_axes,
            )
            for offset in range(taps_count)
        ]
    )


def pointwise(
    mix_rows,
    image_rows,
    cot_rows,
    norm_gain,
    norm_shift,
    up_weight,
    up_bias,
    down_weight,
    down_bias,
    layer_scale,
):
    mix_float = mix_rows.astype(jnp.float32)
    centered = mix_float - jnp.mean(mix_float, axis=-1, keepdims=True)
    inv_dev = lax.rsqrt(jnp.mean(centered * centered, axis=-1, keepdims=True) + EPSILON)
    standardized = centered * inv_dev
    normed = (standardized * norm_gain + norm_shift).astype(jnp.bfloat16)
    pre_act = jnp.dot(normed, up_weight, preferred_element_type=jnp.float32) + up_bias
    activated = activate(pre_act).astype(jnp.bfloat16)
    branch = jnp.dot(activated, down_weight, preferred_element_type=jnp.float32) + down_bias
    cot_float = cot_rows.astype(jnp.float32)
    block_rows = (image_rows.astype(jnp.float32) + layer_scale * branch).astype(jnp.bfloat16)
    branch_cot = cot_float * layer_scale
    branch_grad = branch_cot.astype(jnp.bfloat16)
    act_cot = lax.dot_general(
        branch_grad, down_weight, (((1,), (1,)), ((), ())), preferred_element_type=jnp.float32
    )
    pre_cot = act_cot * activate_slope(pre_act)
    pre_grad = pre_cot.astype(jnp.bfloat16)
    normed_cot = lax.dot_general(
        pre_grad, up_weight, (((1,), (1,)), ((), ())), preferred_element_type=jnp.float32
    )
    scaled_cot = normed_cot * norm_gain
    grad_rows = (
        inv_dev
        * (
            scaled_cot
            - jnp.mean(scaled_cot, axis=-1, keepdims=True)
            - standardized * jnp.mean(scaled_cot * standardized, axis=-1, keepdims=True)
        )
    ).astype(jnp.bfloat16)
    partials = (
        jnp.sum(cot_float * branch, axis=0),
        jnp.sum(branch_cot, axis=0),
        lax.dot_general(
            activated, branch_grad, (((0,), (0,)), ((), ())), preferred_element_type=jnp.float32
        ),
        jnp.sum(pre_cot, axis=0),
        lax.dot_general(
            normed, pre_grad, (((0,), (0,)), ((), ())), preferred_element_type=jnp.float32
        ),
        jnp.sum(normed_cot * standardized, axis=0),
        jnp.sum(normed_cot, axis=0),
    )
    return (block_rows, grad_rows, partials)


def to_columns(band):
    count = lax.axis_size("rows")
    tiles, rows, width, chans = band.shape
    split = band.reshape(tiles, rows, count, width // count, chans).transpose(2, 0, 1, 3, 4)
    split = lax.all_to_all(split, "rows", 0, 0, tiled=True)
    return split.transpose(1, 0, 2, 3, 4).reshape(tiles, count * rows, width // count, chans)


def per_device(
    images,
    cotangent,
    row_taps,
    col_taps,
    norm_gain,
    norm_shift,
    up_weight,
    up_bias,
    down_weight,
    down_bias,
    layer_scale,
):
    tiles_here, band_rows, columns, channels = images.shape
    taps_count = row_taps.shape[0]
    half_reach = (taps_count - 1) // 2
    pixel_scale = 1.0 / math.sqrt(
        tiles_here * lax.axis_size("rep") * band_rows * lax.axis_size("rows") * columns
    )
    image_padded = pad_along(images.astype(jnp.float32), 2, half_reach)
    row_mix = slide_padded(image_padded, row_taps, 2, columns).astype(jnp.bfloat16)
    row_mix = lax.optimization_barrier(row_mix)
    mix_columns = to_columns(row_mix)
    mix_padded = pad_along(mix_columns.astype(jnp.float32), 1, half_reach)
    strip = mix_columns.shape[2]
    parts = 2 if strip % 16 == 0 else 1
    step = strip // parts
    pieces = []
    for part in range(parts):
        local = slide_padded(
            mix_padded[:, :, part * step : (part + 1) * step], col_taps, 1, mix_columns.shape[1]
        ).astype(jnp.bfloat16)
        pieces.append(lax.all_to_all(local, "rows", split_axis=1, concat_axis=2, tiled=True))
    count = lax.axis_size("rows")
    col_mix = jnp.stack(
        [piece.reshape(tiles_here, band_rows, count, step, channels) for piece in pieces], axis=3
    ).reshape(images.shape)
    col_mix = lax.optimization_barrier(col_mix)
    block_rows, grad_rows, partials = pointwise(
        col_mix.reshape(-1, channels),
        images.reshape(-1, channels),
        cotangent.reshape(-1, channels),
        norm_gain,
        norm_shift,
        up_weight,
        up_bias,
        down_weight,
        down_bias,
        layer_scale,
    )
    scale_part, down_bias_part, down_part, up_bias_part, up_part, gain_part, shift_part = partials
    block_out = block_rows.reshape(images.shape)
    grad_rows = lax.optimization_barrier(grad_rows)
    col_grad = grad_rows.reshape(images.shape)
    grad_columns = to_columns(col_grad)
    grad_float = grad_columns.astype(jnp.float32)
    col_part = tap_sums(grad_float, mix_padded, taps_count, 1)
    row_local = slide_padded(
        pad_along(grad_float, 1, half_reach), col_taps[::-1], 1, grad_columns.shape[1]
    ).astype(jnp.bfloat16)
    row_grad = lax.all_to_all(row_local, "rows", split_axis=1, concat_axis=2, tiled=True)
    row_grad = lax.optimization_barrier(row_grad)
    row_part = tap_sums(row_grad, pad_along(images, 2, half_reach), taps_count, 2)
    row_part, row_grad = lax.optimization_barrier((row_part, row_grad))
    image_grad = (
        cotangent.astype(jnp.float32)
        + slide_padded(pad_along(row_grad, 2, half_reach), row_taps[::-1], 2, columns)
    ).astype(jnp.bfloat16)
    down_total, up_total = lax.optimization_barrier(
        lax.psum((down_part * pixel_scale, up_part * pixel_scale), ("rows", "rep"))
    )
    small = (row_part, col_part, scale_part, down_bias_part, up_bias_part, gain_part, shift_part)
    (
        row_total,
        col_total,
        scale_total,
        down_bias_total,
        up_bias_total,
        gain_total,
        shift_total,
    ), image_grad = exchange_sum(tuple(part * pixel_scale for part in small), ("rows", "rep"), image_grad)
    return (
        block_out,
        image_grad,
        row_total,
        col_total,
        scale_total,
        down_bias_total,
        down_total,
        up_bias_total,
        up_total,
        gain_total,
        shift_total,
    )


def exchange_sum(parts, axes, companion):
    count = 1
    for axis in axes:
        count *= lax.axis_size(axis)
    stacked = jnp.concatenate([part.reshape(-1, 128) for part in parts])
    piece = -(-stacked.shape[0] // count)
    stacked = jnp.pad(stacked, ((0, piece * count - stacked.shape[0]), (0, 0)))
    spread = lax.all_to_all(stacked.reshape(count, piece, 128), axes, 0, 0, tiled=True)
    mine = jnp.sum(spread, axis=0, keepdims=True)
    mine, companion = lax.optimization_barrier((mine, companion))
    whole = lax.all_to_all(jnp.broadcast_to(mine, (count, piece, 128)), axes, 0, 0, tiled=True)
    return split_like(whole.reshape(-1), parts), companion


def split_like(flat, parts):
    out = []
    at = 0
    for part in parts:
        out.append(flat[at : at + part.size].reshape(part.shape))
        at += part.size
    return tuple(out)


def solution(mesh):
    placed = (
        P(("groups", "rep"), "rows", None, None),
        P(("groups", "rep"), "rows", None, None),
        P("groups", None),
        P("groups", None),
        P("groups"),
        P("groups"),
        P("groups", None),
        P("groups"),
        P("groups", None),
        P("groups"),
        P("groups"),
    )
    return jax.shard_map(
        per_device,
        mesh=mesh,
        in_specs=placed,
        out_specs=(
            P(("groups", "rep"), "rows", None, None),
            P(("groups", "rep"), "rows", None, None),
            P("groups", None),
            P("groups", None),
            P("groups"),
            P("groups"),
            P("groups", None),
            P("groups"),
            P("groups", None),
            P("groups"),
            P("groups"),
        ),
        check_vma=False,
    )
```

```python
import math

import jax
import jax.numpy as jnp
from jax import lax
from jax.sharding import PartitionSpec as P

EPSILON = 1e-06
CUBIC_TERM = 0.044715
TANH_SCALE = 0.7978845608028654


def activate(pre_act):
    return (
        0.5
        * pre_act
        * (1.0 + jnp.tanh(TANH_SCALE * (pre_act + CUBIC_TERM * pre_act * pre_act * pre_act)))
    )


def activate_slope(pre_act):
    inner = jnp.tanh(TANH_SCALE * (pre_act + CUBIC_TERM * pre_act * pre_act * pre_act))
    return 0.5 * (1.0 + inner) + 0.5 * pre_act * (1.0 - inner * inner) * TANH_SCALE * (
        1.0 + 3.0 * CUBIC_TERM * pre_act * pre_act
    )


def pad_along(source, direction, half_reach):
    widths = [(0, 0)] * source.ndim
    widths[direction] = (half_reach, half_reach)
    return jnp.pad(source, widths)


def slide_padded(padded, taps_table, direction, length):
    shape_out = padded.shape[:direction] + (length,) + padded.shape[direction + 1 :]
    result = jnp.zeros(shape_out, jnp.float32)
    for offset in range(taps_table.shape[0]):
        result = result + taps_table[offset] * lax.slice_in_dim(
            padded, offset, offset + length, axis=direction
        ).astype(jnp.float32)
    return result


def tap_sums(cot_field, padded, taps_count, direction):
    length = cot_field.shape[direction]
    lead_axes = tuple(range(cot_field.ndim - 1))
    return jnp.stack(
        [
            jnp.sum(
                cot_field.astype(jnp.float32)
                * lax.slice_in_dim(padded, offset, offset + length, axis=direction).astype(
                    jnp.float32
                ),
                axis=lead_axes,
            )
            for offset in range(taps_count)
        ]
    )


def pointwise(
    mix_rows,
    image_rows,
    cot_rows,
    norm_gain,
    norm_shift,
    up_weight,
    up_bias,
    down_weight,
    down_bias,
    layer_scale,
):
    mix_float = mix_rows.astype(jnp.float32)
    centered = mix_float - jnp.mean(mix_float, axis=-1, keepdims=True)
    inv_dev = lax.rsqrt(jnp.mean(centered * centered, axis=-1, keepdims=True) + EPSILON)
    standardized = centered * inv_dev
    normed = (standardized * norm_gain + norm_shift).astype(jnp.bfloat16)
    pre_act = jnp.dot(normed, up_weight, preferred_element_type=jnp.float32) + up_bias
    activated = activate(pre_act).astype(jnp.bfloat16)
    branch = jnp.dot(activated, down_weight, preferred_element_type=jnp.float32) + down_bias
    cot_float = cot_rows.astype(jnp.float32)
    block_rows = (image_rows.astype(jnp.float32) + layer_scale * branch).astype(jnp.bfloat16)
    branch_cot = cot_float * layer_scale
    branch_grad = branch_cot.astype(jnp.bfloat16)
    act_cot = lax.dot_general(
        branch_grad, down_weight, (((1,), (1,)), ((), ())), preferred_element_type=jnp.float32
    )
    pre_cot = act_cot * activate_slope(pre_act)
    pre_grad = pre_cot.astype(jnp.bfloat16)
    normed_cot = lax.dot_general(
        pre_grad, up_weight, (((1,), (1,)), ((), ())), preferred_element_type=jnp.float32
    )
    scaled_cot = normed_cot * norm_gain
    grad_rows = (
        inv_dev
        * (
            scaled_cot
            - jnp.mean(scaled_cot, axis=-1, keepdims=True)
            - standardized * jnp.mean(scaled_cot * standardized, axis=-1, keepdims=True)
        )
    ).astype(jnp.bfloat16)
    partials = (
        jnp.sum(cot_float * branch, axis=0),
        jnp.sum(branch_cot, axis=0),
        lax.dot_general(
            activated, branch_grad, (((0,), (0,)), ((), ())), preferred_element_type=jnp.float32
        ),
        jnp.sum(pre_cot, axis=0),
        lax.dot_general(
            normed, pre_grad, (((0,), (0,)), ((), ())), preferred_element_type=jnp.float32
        ),
        jnp.sum(normed_cot * standardized, axis=0),
        jnp.sum(normed_cot, axis=0),
    )
    return (block_rows, grad_rows, partials)


def to_columns(band):
    count = lax.axis_size("rows")
    tiles, rows, width, chans = band.shape
    split = band.reshape(tiles, rows, count, width // count, chans).transpose(2, 0, 1, 3, 4)
    split = lax.all_to_all(split, "rows", 0, 0, tiled=True)
    return split.transpose(1, 0, 2, 3, 4).reshape(tiles, count * rows, width // count, chans)


def per_device(
    images,
    cotangent,
    row_taps,
    col_taps,
    norm_gain,
    norm_shift,
    up_weight,
    up_bias,
    down_weight,
    down_bias,
    layer_scale,
):
    tiles_here, band_rows, columns, channels = images.shape
    taps_count = row_taps.shape[0]
    half_reach = (taps_count - 1) // 2
    pixel_scale = 1.0 / math.sqrt(
        tiles_here * lax.axis_size("rep") * band_rows * lax.axis_size("rows") * columns
    )
    image_padded = pad_along(images.astype(jnp.float32), 2, half_reach)
    row_mix = slide_padded(image_padded, row_taps, 2, columns).astype(jnp.bfloat16)
    row_mix = lax.optimization_barrier(row_mix)
    mix_columns = to_columns(row_mix)
    mix_padded = pad_along(mix_columns.astype(jnp.float32), 1, half_reach)
    strip = mix_columns.shape[2]
    parts = 2 if strip % 16 == 0 else 1
    step = strip // parts
    pieces = []
    for part in range(parts):
        local = slide_padded(
            mix_padded[:, :, part * step : (part + 1) * step], col_taps, 1, mix_columns.shape[1]
        ).astype(jnp.bfloat16)
        pieces.append(lax.all_to_all(local, "rows", split_axis=1, concat_axis=2, tiled=True))
    count = lax.axis_size("rows")
    col_mix = jnp.stack(
        [piece.reshape(tiles_here, band_rows, count, step, channels) for piece in pieces], axis=3
    ).reshape(images.shape)
    col_mix = lax.optimization_barrier(col_mix)
    block_rows, grad_rows, partials = pointwise(
        col_mix.reshape(-1, channels),
        images.reshape(-1, channels),
        cotangent.reshape(-1, channels),
        norm_gain,
        norm_shift,
        up_weight,
        up_bias,
        down_weight,
        down_bias,
        layer_scale,
    )
    scale_part, down_bias_part, down_part, up_bias_part, up_part, gain_part, shift_part = partials
    block_out = block_rows.reshape(images.shape)
    grad_rows = lax.optimization_barrier(grad_rows)
    split_grad = grad_rows.reshape(tiles_here, band_rows, count, strip, channels)
    col_part = None
    row_locals = []
    for part in range(parts):
        grad_columns = to_columns(
            split_grad[:, :, :, part * step : (part + 1) * step].reshape(
                tiles_here, band_rows, count * step, channels
            )
        )
        grad_float = grad_columns.astype(jnp.float32)
        piece_part = tap_sums(
            grad_float, mix_padded[:, :, part * step : (part + 1) * step], taps_count, 1
        )
        col_part = piece_part if col_part is None else col_part + piece_part
        row_locals.append(
            slide_padded(
                pad_along(grad_float, 1, half_reach), col_taps[::-1], 1, grad_columns.shape[1]
            ).astype(jnp.bfloat16)
        )
    row_local = jnp.concatenate(row_locals, axis=2)
    row_grad = lax.all_to_all(row_local, "rows", split_axis=1, concat_axis=2, tiled=True)
    row_grad = lax.optimization_barrier(row_grad)
    row_part = tap_sums(row_grad, pad_along(images, 2, half_reach), taps_count, 2)
    row_part, row_grad = lax.optimization_barrier((row_part, row_grad))
    image_grad = (
        cotangent.astype(jnp.float32)
        + slide_padded(pad_along(row_grad, 2, half_reach), row_taps[::-1], 2, columns)
    ).astype(jnp.bfloat16)
    down_total, up_total = lax.optimization_barrier(
        lax.psum((down_part * pixel_scale, up_part * pixel_scale), ("rows", "rep"))
    )
    small = (row_part, col_part, scale_part, down_bias_part, up_bias_part, gain_part, shift_part)
    (
        row_total,
        col_total,
        scale_total,
        down_bias_total,
        up_bias_total,
        gain_total,
        shift_total,
    ), image_grad = exchange_sum(tuple(part * pixel_scale for part in small), ("rows", "rep"), image_grad)
    return (
        block_out,
        image_grad,
        row_total,
        col_total,
        scale_total,
        down_bias_total,
        down_total,
        up_bias_total,
        up_total,
        gain_total,
        shift_total,
    )


def exchange_sum(parts, axes, companion):
    count = 1
    for axis in axes:
        count *= lax.axis_size(axis)
    stacked = jnp.concatenate([part.reshape(-1, 128) for part in parts])
    piece = -(-stacked.shape[0] // count)
    stacked = jnp.pad(stacked, ((0, piece * count - stacked.shape[0]), (0, 0)))
    spread = lax.all_to_all(stacked.reshape(count, piece, 128), axes, 0, 0, tiled=True)
    mine = jnp.sum(spread, axis=0, keepdims=True)
    mine, companion = lax.optimization_barrier((mine, companion))
    whole = lax.all_to_all(jnp.broadcast_to(mine, (count, piece, 128)), axes, 0, 0, tiled=True)
    return split_like(whole.reshape(-1), parts), companion


def split_like(flat, parts):
    out = []
    at = 0
    for part in parts:
        out.append(flat[at : at + part.size].reshape(part.shape))
        at += part.size
    return tuple(out)


def solution(mesh):
    placed = (
        P(("groups", "rep"), "rows", None, None),
        P(("groups", "rep"), "rows", None, None),
        P("groups", None),
        P("groups", None),
        P("groups"),
        P("groups"),
        P("groups", None),
        P("groups"),
        P("groups", None),
        P("groups"),
        P("groups"),
    )
    return jax.shard_map(
        per_device,
        mesh=mesh,
        in_specs=placed,
        out_specs=(
            P(("groups", "rep"), "rows", None, None),
            P(("groups", "rep"), "rows", None, None),
            P("groups", None),
            P("groups", None),
            P("groups"),
            P("groups"),
            P("groups", None),
            P("groups"),
            P("groups", None),
            P("groups"),
            P("groups"),
        ),
        check_vma=False,
    )
```

```python
import math

import jax
import jax.numpy as jnp
from jax import lax
from jax.sharding import PartitionSpec as P

EPSILON = 1e-06
CUBIC_TERM = 0.044715
TANH_SCALE = 0.7978845608028654


def activate(pre_act):
    return (
        0.5
        * pre_act
        * (1.0 + jnp.tanh(TANH_SCALE * (pre_act + CUBIC_TERM * pre_act * pre_act * pre_act)))
    )


def activate_slope(pre_act):
    inner = jnp.tanh(TANH_SCALE * (pre_act + CUBIC_TERM * pre_act * pre_act * pre_act))
    return 0.5 * (1.0 + inner) + 0.5 * pre_act * (1.0 - inner * inner) * TANH_SCALE * (
        1.0 + 3.0 * CUBIC_TERM * pre_act * pre_act
    )


def pad_along(source, direction, half_reach):
    widths = [(0, 0)] * source.ndim
    widths[direction] = (half_reach, half_reach)
    return jnp.pad(source, widths)


def slide_padded(padded, taps_table, direction, length):
    shape_out = padded.shape[:direction] + (length,) + padded.shape[direction + 1 :]
    result = jnp.zeros(shape_out, jnp.float32)
    for offset in range(taps_table.shape[0]):
        result = result + taps_table[offset] * lax.slice_in_dim(
            padded, offset, offset + length, axis=direction
        ).astype(jnp.float32)
    return result


def tap_sums(cot_field, padded, taps_count, direction):
    length = cot_field.shape[direction]
    lead_axes = tuple(range(cot_field.ndim - 1))
    return jnp.stack(
        [
            jnp.sum(
                cot_field.astype(jnp.float32)
                * lax.slice_in_dim(padded, offset, offset + length, axis=direction).astype(
                    jnp.float32
                ),
                axis=lead_axes,
            )
            for offset in range(taps_count)
        ]
    )


def pointwise(
    mix_rows,
    image_rows,
    cot_rows,
    norm_gain,
    norm_shift,
    up_weight,
    up_bias,
    down_weight,
    down_bias,
    layer_scale,
):
    mix_float = mix_rows.astype(jnp.float32)
    centered = mix_float - jnp.mean(mix_float, axis=-1, keepdims=True)
    inv_dev = lax.rsqrt(jnp.mean(centered * centered, axis=-1, keepdims=True) + EPSILON)
    standardized = centered * inv_dev
    normed = (standardized * norm_gain + norm_shift).astype(jnp.bfloat16)
    pre_act = jnp.dot(normed, up_weight, preferred_element_type=jnp.float32) + up_bias
    activated = activate(pre_act).astype(jnp.bfloat16)
    branch = jnp.dot(activated, down_weight, preferred_element_type=jnp.float32) + down_bias
    cot_float = cot_rows.astype(jnp.float32)
    block_rows = (image_rows.astype(jnp.float32) + layer_scale * branch).astype(jnp.bfloat16)
    branch_cot = cot_float * layer_scale
    branch_grad = branch_cot.astype(jnp.bfloat16)
    act_cot = lax.dot_general(
        branch_grad, down_weight, (((1,), (1,)), ((), ())), preferred_element_type=jnp.float32
    )
    pre_cot = act_cot * activate_slope(pre_act)
    pre_grad = pre_cot.astype(jnp.bfloat16)
    normed_cot = lax.dot_general(
        pre_grad, up_weight, (((1,), (1,)), ((), ())), preferred_element_type=jnp.float32
    )
    scaled_cot = normed_cot * norm_gain
    grad_rows = (
        inv_dev
        * (
            scaled_cot
            - jnp.mean(scaled_cot, axis=-1, keepdims=True)
            - standardized * jnp.mean(scaled_cot * standardized, axis=-1, keepdims=True)
        )
    ).astype(jnp.bfloat16)
    partials = (
        jnp.sum(cot_float * branch, axis=0),
        jnp.sum(branch_cot, axis=0),
        lax.dot_general(
            activated, branch_grad, (((0,), (0,)), ((), ())), preferred_element_type=jnp.float32
        ),
        jnp.sum(pre_cot, axis=0),
        lax.dot_general(
            normed, pre_grad, (((0,), (0,)), ((), ())), preferred_element_type=jnp.float32
        ),
        jnp.sum(normed_cot * standardized, axis=0),
        jnp.sum(normed_cot, axis=0),
    )
    return (block_rows, grad_rows, partials)


def to_columns(band):
    count = lax.axis_size("rows")
    tiles, rows, width, chans = band.shape
    split = band.reshape(tiles, rows, count, width // count, chans).transpose(2, 0, 1, 3, 4)
    split = lax.all_to_all(split, "rows", 0, 0, tiled=True)
    return split.transpose(1, 0, 2, 3, 4).reshape(tiles, count * rows, width // count, chans)


def per_device(
    images,
    cotangent,
    row_taps,
    col_taps,
    norm_gain,
    norm_shift,
    up_weight,
    up_bias,
    down_weight,
    down_bias,
    layer_scale,
):
    tiles_here, band_rows, columns, channels = images.shape
    taps_count = row_taps.shape[0]
    half_reach = (taps_count - 1) // 2
    pixel_scale = 1.0 / math.sqrt(
        tiles_here * lax.axis_size("rep") * band_rows * lax.axis_size("rows") * columns
    )
    bands = 2 if band_rows % 2 == 0 else 1
    band_step = band_rows // bands
    band_pieces = []
    for band in range(bands):
        image_padded = pad_along(
            images[:, band * band_step : (band + 1) * band_step].astype(jnp.float32), 2, half_reach
        )
        row_mix = slide_padded(image_padded, row_taps, 2, columns).astype(jnp.bfloat16)
        row_mix = lax.optimization_barrier(row_mix)
        band_pieces.append(to_columns(row_mix))
    mix_columns = jnp.stack(
        [
            piece.reshape(tiles_here, lax.axis_size("rows"), band_step, piece.shape[2], channels)
            for piece in band_pieces
        ],
        axis=2,
    ).reshape(tiles_here, band_rows * lax.axis_size("rows"), columns // lax.axis_size("rows"), channels)
    mix_padded = pad_along(mix_columns.astype(jnp.float32), 1, half_reach)
    strip = mix_columns.shape[2]
    parts = 2 if strip % 16 == 0 else 1
    step = strip // parts
    pieces = []
    for part in range(parts):
        local = slide_padded(
            mix_padded[:, :, part * step : (part + 1) * step], col_taps, 1, mix_columns.shape[1]
        ).astype(jnp.bfloat16)
        pieces.append(lax.all_to_all(local, "rows", split_axis=1, concat_axis=2, tiled=True))
    count = lax.axis_size("rows")
    col_mix = jnp.stack(
        [piece.reshape(tiles_here, band_rows, count, step, channels) for piece in pieces], axis=3
    ).reshape(images.shape)
    col_mix = lax.optimization_barrier(col_mix)
    block_rows, grad_rows, partials = pointwise(
        col_mix.reshape(-1, channels),
        images.reshape(-1, channels),
        cotangent.reshape(-1, channels),
        norm_gain,
        norm_shift,
        up_weight,
        up_bias,
        down_weight,
        down_bias,
        layer_scale,
    )
    scale_part, down_bias_part, down_part, up_bias_part, up_part, gain_part, shift_part = partials
    block_out = block_rows.reshape(images.shape)
    grad_rows = lax.optimization_barrier(grad_rows)
    col_grad = grad_rows.reshape(images.shape)
    grad_columns = to_columns(col_grad)
    grad_float = grad_columns.astype(jnp.float32)
    col_part = tap_sums(grad_float, mix_padded, taps_count, 1)
    row_local = slide_padded(
        pad_along(grad_float, 1, half_reach), col_taps[::-1], 1, grad_columns.shape[1]
    ).astype(jnp.bfloat16)
    row_grad = lax.all_to_all(row_local, "rows", split_axis=1, concat_axis=2, tiled=True)
    row_grad = lax.optimization_barrier(row_grad)
    row_part = tap_sums(row_grad, pad_along(images, 2, half_reach), taps_count, 2)
    row_part, row_grad = lax.optimization_barrier((row_part, row_grad))
    image_grad = (
        cotangent.astype(jnp.float32)
        + slide_padded(pad_along(row_grad, 2, half_reach), row_taps[::-1], 2, columns)
    ).astype(jnp.bfloat16)
    down_total, up_total = lax.optimization_barrier(
        lax.psum((down_part * pixel_scale, up_part * pixel_scale), ("rows", "rep"))
    )
    small = (row_part, col_part, scale_part, down_bias_part, up_bias_part, gain_part, shift_part)
    (
        row_total,
        col_total,
        scale_total,
        down_bias_total,
        up_bias_total,
        gain_total,
        shift_total,
    ), image_grad = exchange_sum(tuple(part * pixel_scale for part in small), ("rows", "rep"), image_grad)
    return (
        block_out,
        image_grad,
        row_total,
        col_total,
        scale_total,
        down_bias_total,
        down_total,
        up_bias_total,
        up_total,
        gain_total,
        shift_total,
    )


def exchange_sum(parts, axes, companion):
    count = 1
    for axis in axes:
        count *= lax.axis_size(axis)
    stacked = jnp.concatenate([part.reshape(-1, 128) for part in parts])
    piece = -(-stacked.shape[0] // count)
    stacked = jnp.pad(stacked, ((0, piece * count - stacked.shape[0]), (0, 0)))
    spread = lax.all_to_all(stacked.reshape(count, piece, 128), axes, 0, 0, tiled=True)
    mine = jnp.sum(spread, axis=0, keepdims=True)
    mine, companion = lax.optimization_barrier((mine, companion))
    whole = lax.all_to_all(jnp.broadcast_to(mine, (count, piece, 128)), axes, 0, 0, tiled=True)
    return split_like(whole.reshape(-1), parts), companion


def split_like(flat, parts):
    out = []
    at = 0
    for part in parts:
        out.append(flat[at : at + part.size].reshape(part.shape))
        at += part.size
    return tuple(out)


def solution(mesh):
    placed = (
        P(("groups", "rep"), "rows", None, None),
        P(("groups", "rep"), "rows", None, None),
        P("groups", None),
        P("groups", None),
        P("groups"),
        P("groups"),
        P("groups", None),
        P("groups"),
        P("groups", None),
        P("groups"),
        P("groups"),
    )
    return jax.shard_map(
        per_device,
        mesh=mesh,
        in_specs=placed,
        out_specs=(
            P(("groups", "rep"), "rows", None, None),
            P(("groups", "rep"), "rows", None, None),
            P("groups", None),
            P("groups", None),
            P("groups"),
            P("groups"),
            P("groups", None),
            P("groups"),
            P("groups", None),
            P("groups"),
            P("groups"),
        ),
        check_vma=False,
    )
```

```python
import math

import jax
import jax.numpy as jnp
from jax import lax
from jax.sharding import PartitionSpec as P

EPSILON = 1e-06
CUBIC_TERM = 0.044715
TANH_SCALE = 0.7978845608028654


def activate(pre_act):
    return (
        0.5
        * pre_act
        * (1.0 + jnp.tanh(TANH_SCALE * (pre_act + CUBIC_TERM * pre_act * pre_act * pre_act)))
    )


def activate_slope(pre_act):
    inner = jnp.tanh(TANH_SCALE * (pre_act + CUBIC_TERM * pre_act * pre_act * pre_act))
    return 0.5 * (1.0 + inner) + 0.5 * pre_act * (1.0 - inner * inner) * TANH_SCALE * (
        1.0 + 3.0 * CUBIC_TERM * pre_act * pre_act
    )


def pad_along(source, direction, half_reach):
    widths = [(0, 0)] * source.ndim
    widths[direction] = (half_reach, half_reach)
    return jnp.pad(source, widths)


def slide_padded(padded, taps_table, direction, length):
    shape_out = padded.shape[:direction] + (length,) + padded.shape[direction + 1 :]
    result = jnp.zeros(shape_out, jnp.float32)
    for offset in range(taps_table.shape[0]):
        result = result + taps_table[offset] * lax.slice_in_dim(
            padded, offset, offset + length, axis=direction
        ).astype(jnp.float32)
    return result


def tap_sums(cot_field, padded, taps_count, direction):
    length = cot_field.shape[direction]
    lead_axes = tuple(range(cot_field.ndim - 1))
    return jnp.stack(
        [
            jnp.sum(
                cot_field.astype(jnp.float32)
                * lax.slice_in_dim(padded, offset, offset + length, axis=direction).astype(
                    jnp.float32
                ),
                axis=lead_axes,
            )
            for offset in range(taps_count)
        ]
    )


def pointwise(
    mix_rows,
    image_rows,
    cot_rows,
    norm_gain,
    norm_shift,
    up_weight,
    up_bias,
    down_weight,
    down_bias,
    layer_scale,
):
    mix_float = mix_rows.astype(jnp.float32)
    centered = mix_float - jnp.mean(mix_float, axis=-1, keepdims=True)
    inv_dev = lax.rsqrt(jnp.mean(centered * centered, axis=-1, keepdims=True) + EPSILON)
    standardized = centered * inv_dev
    normed = (standardized * norm_gain + norm_shift).astype(jnp.bfloat16)
    pre_act = jnp.dot(normed, up_weight, preferred_element_type=jnp.float32) + up_bias
    activated = activate(pre_act).astype(jnp.bfloat16)
    branch = jnp.dot(activated, down_weight, preferred_element_type=jnp.float32) + down_bias
    cot_float = cot_rows.astype(jnp.float32)
    block_rows = (image_rows.astype(jnp.float32) + layer_scale * branch).astype(jnp.bfloat16)
    branch_cot = cot_float * layer_scale
    branch_grad = branch_cot.astype(jnp.bfloat16)
    act_cot = lax.dot_general(
        branch_grad, down_weight, (((1,), (1,)), ((), ())), preferred_element_type=jnp.float32
    )
    pre_cot = act_cot * activate_slope(pre_act)
    pre_grad = pre_cot.astype(jnp.bfloat16)
    normed_cot = lax.dot_general(
        pre_grad, up_weight, (((1,), (1,)), ((), ())), preferred_element_type=jnp.float32
    )
    scaled_cot = normed_cot * norm_gain
    grad_rows = (
        inv_dev
        * (
            scaled_cot
            - jnp.mean(scaled_cot, axis=-1, keepdims=True)
            - standardized * jnp.mean(scaled_cot * standardized, axis=-1, keepdims=True)
        )
    ).astype(jnp.bfloat16)
    partials = (
        jnp.sum(cot_float * branch, axis=0),
        jnp.sum(branch_cot, axis=0),
        lax.dot_general(
            activated, branch_grad, (((0,), (0,)), ((), ())), preferred_element_type=jnp.float32
        ),
        jnp.sum(pre_cot, axis=0),
        lax.dot_general(
            normed, pre_grad, (((0,), (0,)), ((), ())), preferred_element_type=jnp.float32
        ),
        jnp.sum(normed_cot * standardized, axis=0),
        jnp.sum(normed_cot, axis=0),
    )
    return (block_rows, grad_rows, partials)


def to_columns(band):
    count = lax.axis_size("rows")
    tiles, rows, width, chans = band.shape
    split = band.reshape(tiles, rows, count, width // count, chans).transpose(2, 0, 1, 3, 4)
    split = lax.all_to_all(split, "rows", 0, 0, tiled=True)
    return split.transpose(1, 0, 2, 3, 4).reshape(tiles, count * rows, width // count, chans)


def per_device(
    images,
    cotangent,
    row_taps,
    col_taps,
    norm_gain,
    norm_shift,
    up_weight,
    up_bias,
    down_weight,
    down_bias,
    layer_scale,
):
    tiles_here, band_rows, columns, channels = images.shape
    taps_count = row_taps.shape[0]
    half_reach = (taps_count - 1) // 2
    pixel_scale = 1.0 / math.sqrt(
        tiles_here * lax.axis_size("rep") * band_rows * lax.axis_size("rows") * columns
    )
    bands = 2 if band_rows % 2 == 0 else 1
    band_step = band_rows // bands
    band_pieces = []
    for band in range(bands):
        image_padded = pad_along(
            images[:, band * band_step : (band + 1) * band_step].astype(jnp.float32), 2, half_reach
        )
        row_mix = slide_padded(image_padded, row_taps, 2, columns).astype(jnp.bfloat16)
        row_mix = lax.optimization_barrier(row_mix)
        band_pieces.append(to_columns(row_mix))
    mix_columns = jnp.stack(
        [
            piece.reshape(tiles_here, lax.axis_size("rows"), band_step, piece.shape[2], channels)
            for piece in band_pieces
        ],
        axis=2,
    ).reshape(tiles_here, band_rows * lax.axis_size("rows"), columns // lax.axis_size("rows"), channels)
    mix_padded = pad_along(mix_columns.astype(jnp.float32), 1, half_reach)
    strip = mix_columns.shape[2]
    parts = 4 if strip % 32 == 0 else (2 if strip % 16 == 0 else 1)
    step = strip // parts
    pieces = []
    for part in range(parts):
        local = slide_padded(
            mix_padded[:, :, part * step : (part + 1) * step], col_taps, 1, mix_columns.shape[1]
        ).astype(jnp.bfloat16)
        pieces.append(lax.all_to_all(local, "rows", split_axis=1, concat_axis=2, tiled=True))
    count = lax.axis_size("rows")
    col_mix = jnp.stack(
        [piece.reshape(tiles_here, band_rows, count, step, channels) for piece in pieces], axis=3
    ).reshape(images.shape)
    col_mix = lax.optimization_barrier(col_mix)
    block_rows, grad_rows, partials = pointwise(
        col_mix.reshape(-1, channels),
        images.reshape(-1, channels),
        cotangent.reshape(-1, channels),
        norm_gain,
        norm_shift,
        up_weight,
        up_bias,
        down_weight,
        down_bias,
        layer_scale,
    )
    scale_part, down_bias_part, down_part, up_bias_part, up_part, gain_part, shift_part = partials
    block_out = block_rows.reshape(images.shape)
    grad_rows = lax.optimization_barrier(grad_rows)
    col_grad = grad_rows.reshape(images.shape)
    grad_columns = to_columns(col_grad)
    grad_float = grad_columns.astype(jnp.float32)
    col_part = tap_sums(grad_float, mix_padded, taps_count, 1)
    row_local = slide_padded(
        pad_along(grad_float, 1, half_reach), col_taps[::-1], 1, grad_columns.shape[1]
    ).astype(jnp.bfloat16)
    row_grad = lax.all_to_all(row_local, "rows", split_axis=1, concat_axis=2, tiled=True)
    row_grad = lax.optimization_barrier(row_grad)
    row_part = tap_sums(row_grad, pad_along(images, 2, half_reach), taps_count, 2)
    row_part, row_grad = lax.optimization_barrier((row_part, row_grad))
    image_grad = (
        cotangent.astype(jnp.float32)
        + slide_padded(pad_along(row_grad, 2, half_reach), row_taps[::-1], 2, columns)
    ).astype(jnp.bfloat16)
    down_total, up_total = lax.optimization_barrier(
        lax.psum((down_part * pixel_scale, up_part * pixel_scale), ("rows", "rep"))
    )
    small = (row_part, col_part, scale_part, down_bias_part, up_bias_part, gain_part, shift_part)
    (
        row_total,
        col_total,
        scale_total,
        down_bias_total,
        up_bias_total,
        gain_total,
        shift_total,
    ), image_grad = exchange_sum(tuple(part * pixel_scale for part in small), ("rows", "rep"), image_grad)
    return (
        block_out,
        image_grad,
        row_total,
        col_total,
        scale_total,
        down_bias_total,
        down_total,
        up_bias_total,
        up_total,
        gain_total,
        shift_total,
    )


def exchange_sum(parts, axes, companion):
    count = 1
    for axis in axes:
        count *= lax.axis_size(axis)
    stacked = jnp.concatenate([part.reshape(-1, 128) for part in parts])
    piece = -(-stacked.shape[0] // count)
    stacked = jnp.pad(stacked, ((0, piece * count - stacked.shape[0]), (0, 0)))
    spread = lax.all_to_all(stacked.reshape(count, piece, 128), axes, 0, 0, tiled=True)
    mine = jnp.sum(spread, axis=0, keepdims=True)
    mine, companion = lax.optimization_barrier((mine, companion))
    whole = lax.all_to_all(jnp.broadcast_to(mine, (count, piece, 128)), axes, 0, 0, tiled=True)
    return split_like(whole.reshape(-1), parts), companion


def split_like(flat, parts):
    out = []
    at = 0
    for part in parts:
        out.append(flat[at : at + part.size].reshape(part.shape))
        at += part.size
    return tuple(out)


def solution(mesh):
    placed = (
        P(("groups", "rep"), "rows", None, None),
        P(("groups", "rep"), "rows", None, None),
        P("groups", None),
        P("groups", None),
        P("groups"),
        P("groups"),
        P("groups", None),
        P("groups"),
        P("groups", None),
        P("groups"),
        P("groups"),
    )
    return jax.shard_map(
        per_device,
        mesh=mesh,
        in_specs=placed,
        out_specs=(
            P(("groups", "rep"), "rows", None, None),
            P(("groups", "rep"), "rows", None, None),
            P("groups", None),
            P("groups", None),
            P("groups"),
            P("groups"),
            P("groups", None),
            P("groups"),
            P("groups", None),
            P("groups"),
            P("groups"),
        ),
        check_vma=False,
    )
```
